512 devices in a mesh: lat: 16 (over x, y_lo), lon: 32 (over z, y_hi, core).
Axes of the slice: x: 4, y: 8 (y_hi: 2, y_lo: 4; y = y_hi * 4 + y_lo), z: 8, core: 2. Of those that a mesh axis runs over, the one named last changes fastest.
Arguments:
- base_state: float32 [8, 2, 1920, 4096], P(None, None, 'lat', 'lon'), may hold values from -6 to 6
- section_state: float32 [8, 2, 1920, 4096], P(None, None, 'lat', 'lon'), may hold values from -6 to 6
- cutoff: int32 [1920], replicated, may hold values from 8 to 64, as said below
- filter_mask: int32 [1920], replicated, may hold values from 0 to 1, as said below
Outputs:
- new_state: float32 [8, 2, 1920, 4096], P(None, None, 'lat', 'lon')
The draws below stay inside these ranges and needn't reach their ends.
Inputs may be any that keep to these rules, and one draw needn't show every extreme that they name: `cutoff`: every value lies in 8 to 64, and 64 occurs in every draw. `filter_mask`: 1 exactly on a run of rows starting at each pole, 0 elsewhere; each run holds 1 to 480 rows, and one of the two runs holds exactly 480.
All inputs are finite; a program needn't handle non-finite values.
Results may differ from the reference program's by a relative error of at most 0.0003.
Values sent between devices are 32-bit elements; how exact they have to be, the bound alone decides.
No kernel may reach another device: no remote copies, remote signals or barrier semaphores. Data moves between devices by JAX's collectives and lax.ppermute only.
A program may use at most 64 MiB of HBM per device.

```python
import jax
import jax.numpy as jnp
from jax import lax

F = 8
LEV = 2
KMAX = 64
NLAT = 1920
NLON = 4096


def draw_cutoff(key, part):
    first_key, second_key = jax.random.split(jax.random.fold_in(key, 11))
    lowest = max(1, KMAX // 8)
    drawn = jax.random.randint(first_key, (NLAT,), lowest, KMAX + 1)
    where_top = jax.random.randint(second_key, (), 0, NLAT)
    return drawn.at[where_top].set(KMAX).astype(jnp.int32)


def draw_filter_mask(key, part):
    first_key, second_key = jax.random.split(jax.random.fold_in(key, 23))
    quarter_rows = NLAT // 4
    other_width = jax.random.randint(first_key, (), 1, quarter_rows + 1)
    which_pole = jax.random.randint(second_key, (), 0, 2)
    south_width = jnp.where(which_pole == 0, quarter_rows, other_width)
    north_width = jnp.where(which_pole == 0, other_width, quarter_rows)
    row_index = jnp.arange(NLAT, dtype=jnp.int32)
    chosen = (row_index < south_width) | (row_index >= NLAT - north_width)
    return chosen.astype(jnp.int32)


def levels(rng, extent, pieces, low, largest):
    gain = 1.0
    for position, blocks in pieces:
        steps = jax.random.uniform(jax.random.fold_in(jax.random.fold_in(rng, 6), position), (blocks,), jnp.float32, low / len(pieces), largest / len(pieces))
        gain = gain * jnp.repeat(jnp.exp(steps), extent[position] // blocks).reshape((-1,) + (1,) * (len(extent) - 1 - position))
    return gain


def noise(rng, dims, spread, reach, shards=(), kind=jnp.bfloat16):
    entries = spread * jax.random.normal(rng, dims, jnp.float32)
    if shards:
        entries = entries * levels(rng, dims, shards, -0.22, 0.18)
    return jnp.clip(entries, -reach, reach).astype(kind)


def setup_inputs(seed: int = 0) -> dict:
    splits = jax.random.split(jax.random.key(seed), 5)
    base_state = noise(splits[0], (F, LEV, NLAT, NLON), 1.0, 6.0, ((2, 16), (3, 32)), jnp.float32)
    section_state = noise(splits[1], (F, LEV, NLAT, NLON), 1.0, 6.0, ((2, 16), (3, 32)), jnp.float32)
    cutoff = draw_cutoff(jax.random.fold_in(splits[4], 71), 0)
    filter_mask = draw_filter_mask(jax.random.fold_in(splits[4], 71), 0)
    return {"base_state": base_state, "section_state": section_state, "cutoff": cutoff, "filter_mask": filter_mask}


section_weight = 0.4


def interface(padded, along):
    length = padded.shape[along]
    outer_low = lax.slice_in_dim(padded, 0, length - 3, axis=along)
    inner_low = lax.slice_in_dim(padded, 1, length - 2, axis=along)
    inner_high = lax.slice_in_dim(padded, 2, length - 1, axis=along)
    outer_high = lax.slice_in_dim(padded, 3, length, axis=along)
    return (7.0 * (inner_low + inner_high) - (outer_low + outer_high)) / 12.0


def cell_cosine(first_row, row_count, total_rows):
    index_rows = first_row + jnp.arange(row_count, dtype=jnp.int32)
    return jnp.sin(jnp.pi * (index_rows.astype(jnp.float32) + 0.5) / total_rows)


def face_cosine(first_row, row_count, total_rows):
    index_faces = first_row + jnp.arange(row_count + 1, dtype=jnp.int32)
    raw_values = jnp.sin(jnp.pi * index_faces.astype(jnp.float32) / total_rows)
    return jnp.where((index_faces == 0) | (index_faces == total_rows), 0.0, raw_values)


def pad_rows(field, flip_sign):
    total_rows = field.shape[1]
    half_cols = field.shape[2] // 2
    padded = jnp.pad(field, ((0, 0), (2, 2), (0, 0)))
    south_row = flip_sign * jnp.roll(field[:, 0], half_cols, axis=-1)
    north_row = flip_sign * jnp.roll(field[:, -1], half_cols, axis=-1)
    return padded.at[:, 1].set(south_row).at[:, total_rows + 2].set(north_row)


def pad_cols(field):
    return jnp.concatenate([field[..., -2:], field, field[..., :2]], axis=-1)


def reference(base_state, section_state, cutoff, filter_mask):
    face_cos = face_cosine(0, NLAT, NLAT)
    cell_cos = cell_cosine(0, NLAT, NLAT)
    u_faces = interface(pad_cols(section_state[0]), 2)
    v_faces = interface(pad_rows(section_state[1], -1.0), 1)
    kept_modes = jnp.arange(NLON // 2 + 1, dtype=jnp.int32)[None, :] < cutoff[:, None]
    rows_kept = filter_mask[:, None] == 1

    def per_field(field_index):
        field = lax.dynamic_index_in_dim(section_state, field_index, 0, keepdims=False)
        flip_sign = jnp.where(field_index < 2, -1.0, 1.0).astype(section_state.dtype)
        north_flux = v_faces * interface(pad_rows(field, flip_sign), 1) * face_cos[None, :, None]
        east_flux = u_faces * interface(pad_cols(field), 2)
        tendency = -((east_flux[..., 1:] - east_flux[..., :-1]) + (north_flux[:, 1:] - north_flux[:, :-1])) / cell_cos[None, :, None]
        spectrum = jnp.fft.rfft(tendency, axis=-1)
        smooth = jnp.fft.irfft(spectrum * kept_modes[None], n=NLON, axis=-1).astype(tendency.dtype)
        filtered = jnp.where(rows_kept[None], smooth, tendency)
        starting = lax.dynamic_index_in_dim(base_state, field_index, 0, keepdims=False)
        return starting + section_weight * filtered

    return lax.map(per_field, jnp.arange(F, dtype=jnp.int32))
```

```python
import jax
import jax.numpy as jnp
from jax import lax
from jax.sharding import PartitionSpec as P

KMAX = 64


section_weight = 0.4


def passed_along(block, axis, distance):
    devices = range(lax.axis_size(axis))
    route = [((i - distance) % len(devices), i) for i in devices]
    return lax.ppermute(block, axis, route)


def padded_2(block, sides, width, periodic):
    for axis, dim in sides:
        count = lax.axis_size(axis)
        forward = [(i, i + 1) for i in range(count - 1)]
        if periodic:
            forward.append((count - 1, 0))
        backward = [(target, source) for source, target in forward]
        low = lax.ppermute(
            lax.slice_in_dim(block, block.shape[dim] - width, None, axis=dim), axis, forward
        )
        high = lax.ppermute(lax.slice_in_dim(block, 0, width, axis=dim), axis, backward)
        block = jnp.concatenate([low, block, high], axis=dim)
    return block


def interface(padded, along):
    length = padded.shape[along]
    outer_low = lax.slice_in_dim(padded, 0, length - 3, axis=along)
    inner_low = lax.slice_in_dim(padded, 1, length - 2, axis=along)
    inner_high = lax.slice_in_dim(padded, 2, length - 1, axis=along)
    outer_high = lax.slice_in_dim(padded, 3, length, axis=along)
    return (7.0 * (inner_low + inner_high) - (outer_low + outer_high)) / 12.0


def cell_cosine(first_row, row_count, total_rows):
    index_rows = first_row + jnp.arange(row_count, dtype=jnp.int32)
    return jnp.sin(jnp.pi * (index_rows.astype(jnp.float32) + 0.5) / total_rows)


def face_cosine(first_row, row_count, total_rows):
    index_faces = first_row + jnp.arange(row_count + 1, dtype=jnp.int32)
    raw_values = jnp.sin(jnp.pi * index_faces.astype(jnp.float32) / total_rows)
    return jnp.where((index_faces == 0) | (index_faces == total_rows), 0.0, raw_values)


def local_basis(first_col, col_count, total_cols):
    positions = first_col + jnp.arange(col_count, dtype=jnp.int32)
    product_index = positions[:, None] * jnp.arange(KMAX, dtype=jnp.int32)[None, :] % total_cols
    phases = product_index.astype(jnp.float32) * (2.0 * jnp.pi / total_cols)
    return jnp.concatenate([jnp.cos(phases), jnp.sin(phases)], axis=1)


def mode_weights(cut_rows, total_cols):
    mode_index = jnp.arange(2 * KMAX, dtype=jnp.int32) % KMAX
    mode_scale = jnp.where(mode_index == 0, 1.0 / total_cols, 2.0 / total_cols).astype(jnp.float32)
    return jnp.where(mode_index[None, :] < cut_rows[:, None], mode_scale[None, :], 0.0)


def run_filter(row_values, cut_rows, first_col, total_cols):
    fields, levels, row_count, col_count = row_values.shape
    basis = local_basis(first_col, col_count, total_cols)
    flat = row_values.reshape(fields * levels, row_count, col_count)
    partial = jnp.einsum("arn,nk->ark", flat, basis, precision=lax.Precision.HIGHEST)
    coefficients = lax.psum(partial, "lon")
    weighted = coefficients * mode_weights(cut_rows, total_cols)[None]
    smooth = jnp.einsum("ark,nk->arn", weighted, basis, precision=lax.Precision.HIGHEST)
    return smooth.reshape(fields, levels, row_count, col_count)


def local(base_state, section_state, cutoff, filter_mask):
    fields, levels, row_count, col_count = section_state.shape
    lat_count = lax.axis_size("lat")
    lon_count = lax.axis_size("lon")
    band_index = lax.axis_index("lat")
    total_rows = row_count * lat_count
    total_cols = col_count * lon_count
    first_row = band_index * row_count
    flip_sign = jnp.where(jnp.arange(fields) < 2, -1.0, 1.0).astype(jnp.float32)[:, None, None]
    polar_edge = jnp.where(
        band_index == 0, section_state[:, :, 0, :], section_state[:, :, row_count - 1, :]
    )
    crossed = passed_along(polar_edge, "lon", lon_count // 2) * flip_sign
    lat_padded = padded_2(section_state, (("lat", 2),), 2, False)
    south_row = jnp.where(band_index == 0, crossed, lat_padded[:, :, 1, :])
    north_row = jnp.where(band_index == lat_count - 1, crossed, lat_padded[:, :, row_count + 2, :])
    lat_padded = lat_padded.at[:, :, 1, :].set(south_row).at[:, :, row_count + 2, :].set(north_row)
    lon_padded = padded_2(section_state, (("lon", 3),), 2, True)
    face_cos = face_cosine(first_row, row_count, total_rows)
    cell_cos = cell_cosine(first_row, row_count, total_rows)
    lat_faces = interface(lat_padded, 2)
    lon_faces = interface(lon_padded, 3)
    north_flux = lat_faces[1][None] * lat_faces * face_cos[None, None, :, None]
    east_flux = lon_faces[0][None] * lon_faces
    tendency = (
        -(east_flux[..., 1:] - east_flux[..., :-1] + (north_flux[:, :, 1:] - north_flux[:, :, :-1]))
        / cell_cos[None, None, :, None]
    )
    own_mask = lax.dynamic_slice_in_dim(filter_mask, first_row, row_count)
    cut_rows = lax.dynamic_slice_in_dim(cutoff, first_row, row_count)
    smooth = run_filter(tendency, cut_rows, lax.axis_index("lon") * col_count, total_cols)
    filtered = jnp.where(own_mask[None, None, :, None] == 1, smooth, tendency)
    return base_state + section_weight * filtered


def solution(mesh):
    placed = (P(None, None, "lat", "lon"), P(None, None, "lat", "lon"), P(), P())
    return jax.shard_map(
        local, mesh=mesh, in_specs=placed, out_specs=P(None, None, "lat", "lon"), check_vma=False
    )
```

```python
import jax
import jax.numpy as jnp
from jax import lax
from jax.sharding import PartitionSpec as P

KMAX = 64
LON = ("lonc", "core")


section_weight = 0.4


def passed_along(block, axis, distance):
    devices = range(lax.axis_size(axis))
    route = [((i - distance) % len(devices), i) for i in devices]
    return lax.ppermute(block, axis, route)


def padded_2(block, sides, width, periodic):
    for axis, dim in sides:
        count = lax.axis_size(axis)
        forward = [(i, i + 1) for i in range(count - 1)]
        if periodic:
            forward.append((count - 1, 0))
        backward = [(target, source) for source, target in forward]
        low = lax.ppermute(
            lax.slice_in_dim(block, block.shape[dim] - width, None, axis=dim), axis, forward
        )
        high = lax.ppermute(lax.slice_in_dim(block, 0, width, axis=dim), axis, backward)
        block = jnp.concatenate([low, block, high], axis=dim)
    return block


def interface(padded, along):
    length = padded.shape[along]
    outer_low = lax.slice_in_dim(padded, 0, length - 3, axis=along)
    inner_low = lax.slice_in_dim(padded, 1, length - 2, axis=along)
    inner_high = lax.slice_in_dim(padded, 2, length - 1, axis=along)
    outer_high = lax.slice_in_dim(padded, 3, length, axis=along)
    return (7.0 * (inner_low + inner_high) - (outer_low + outer_high)) / 12.0


def cell_cosine(first_row, row_count, total_rows):
    index_rows = first_row + jnp.arange(row_count, dtype=jnp.int32)
    return jnp.sin(jnp.pi * (index_rows.astype(jnp.float32) + 0.5) / total_rows)


def face_cosine(first_row, row_count, total_rows):
    index_faces = first_row + jnp.arange(row_count + 1, dtype=jnp.int32)
    raw_values = jnp.sin(jnp.pi * index_faces.astype(jnp.float32) / total_rows)
    return jnp.where((index_faces == 0) | (index_faces == total_rows), 0.0, raw_values)


def local_basis(first_col, col_count, total_cols):
    positions = first_col + jnp.arange(col_count, dtype=jnp.int32)
    product_index = positions[:, None] * jnp.arange(KMAX, dtype=jnp.int32)[None, :] % total_cols
    phases = product_index.astype(jnp.float32) * (2.0 * jnp.pi / total_cols)
    return jnp.concatenate([jnp.cos(phases), jnp.sin(phases)], axis=1)


def mode_weights(cut_rows, total_cols):
    mode_index = jnp.arange(2 * KMAX, dtype=jnp.int32) % KMAX
    mode_scale = jnp.where(mode_index == 0, 1.0 / total_cols, 2.0 / total_cols).astype(jnp.float32)
    return jnp.where(mode_index[None, :] < cut_rows[:, None], mode_scale[None, :], 0.0)


def swap_halves(block, core_index):
    half = block.shape[0] // 2
    low, high = block[:half], block[half:]
    keep = jnp.where(core_index == 0, low, high)
    give = jnp.where(core_index == 0, high, low)
    return keep, lax.ppermute(give, "core", [(0, 1), (1, 0)])


def run_filter(row_values, cut_rows, first_col, total_cols):
    fields, levels, row_count, col_count = row_values.shape
    chips = lax.axis_size("lonc")
    core_index = lax.axis_index("core")
    basis = local_basis(first_col, col_count, total_cols)
    flat = row_values.reshape(fields * levels * row_count, col_count)
    partial = jnp.dot(flat, basis, precision=lax.Precision.HIGHEST)
    keep, got = swap_halves(partial, core_index)
    chip_sum = (keep + got).reshape(chips, -1, 2 * KMAX)
    pieces = lax.all_to_all(chip_sum, "lonc", 0, 0, tiled=True)
    reduced = jnp.sum(pieces, axis=0)
    spread = jnp.broadcast_to(reduced[None], (chips,) + reduced.shape)
    gathered = lax.all_to_all(spread, "lonc", 0, 0, tiled=True).reshape(-1, 2 * KMAX)
    other = lax.ppermute(gathered, "core", [(0, 1), (1, 0)])
    low = jnp.where(core_index == 0, gathered, other)
    high = jnp.where(core_index == 0, other, gathered)
    coefficients = jnp.concatenate([low, high], axis=0).reshape(fields * levels, row_count, 2 * KMAX)
    weighted = coefficients * mode_weights(cut_rows, total_cols)[None]
    smooth = jnp.dot(weighted.reshape(-1, 2 * KMAX), basis.T, precision=lax.Precision.HIGHEST)
    return smooth.reshape(fields, levels, row_count, col_count)


def local(base_state, section_state, cutoff, filter_mask):
    fields, levels, row_count, col_count = section_state.shape
    lat_count = lax.axis_size("lat")
    lon_count = lax.axis_size("lonc") * lax.axis_size("core")
    lon_index = lax.axis_index("lonc") * lax.axis_size("core") + lax.axis_index("core")
    band_index = lax.axis_index("lat")
    total_rows = row_count * lat_count
    total_cols = col_count * lon_count
    first_row = band_index * row_count
    flip_sign = jnp.where(jnp.arange(fields) < 2, -1.0, 1.0).astype(jnp.float32)[:, None, None]
    polar_edge = jnp.where(
        band_index == 0, section_state[:, :, 0, :], section_state[:, :, row_count - 1, :]
    )
    crossed = passed_along(polar_edge, LON, lon_count // 2) * flip_sign
    lat_padded = padded_2(section_state, (("lat", 2),), 2, False)
    south_row = jnp.where(band_index == 0, crossed, lat_padded[:, :, 1, :])
    north_row = jnp.where(band_index == lat_count - 1, crossed, lat_padded[:, :, row_count + 2, :])
    lat_padded = lat_padded.at[:, :, 1, :].set(south_row).at[:, :, row_count + 2, :].set(north_row)
    lon_padded = padded_2(section_state, ((LON, 3),), 2, True)
    face_cos = face_cosine(first_row, row_count, total_rows)
    cell_cos = cell_cosine(first_row, row_count, total_rows)
    lat_faces = interface(lat_padded, 2)
    lon_faces = interface(lon_padded, 3)
    north_flux = lat_faces[1][None] * lat_faces * face_cos[None, None, :, None]
    east_flux = lon_faces[0][None] * lon_faces
    tendency = (
        -(east_flux[..., 1:] - east_flux[..., :-1] + (north_flux[:, :, 1:] - north_flux[:, :, :-1]))
        / cell_cos[None, None, :, None]
    )
    own_mask = lax.dynamic_slice_in_dim(filter_mask, first_row, row_count)
    cut_rows = lax.dynamic_slice_in_dim(cutoff, first_row, row_count)
    smooth = run_filter(tendency, cut_rows, lon_index * col_count, total_cols)
    filtered = jnp.where(own_mask[None, None, :, None] == 1, smooth, tendency)
    return base_state + section_weight * filtered


def solution(mesh):
    chips = mesh.shape["lon"] // 2
    mesh = jax.sharding.Mesh(mesh.devices.reshape(mesh.shape["lat"], chips, 2), ("lat", "lonc", "core"))
    placed = (P(None, None, "lat", LON), P(None, None, "lat", LON), P(), P())
    return jax.shard_map(
        local, mesh=mesh, in_specs=placed, out_specs=P(None, None, "lat", LON), check_vma=False
    )
```

```python
import jax
import jax.numpy as jnp
from jax import lax
from jax.sharding import PartitionSpec as P

KMAX = 64
LON = ("ring", "pair", "core")


section_weight = 0.4


def passed_along(block, axis, distance):
    devices = range(lax.axis_size(axis))
    route = [((i - distance) % len(devices), i) for i in devices]
    return lax.ppermute(block, axis, route)


def padded_2(block, sides, width, periodic):
    for axis, dim in sides:
        count = lax.axis_size(axis)
        forward = [(i, i + 1) for i in range(count - 1)]
        if periodic:
            forward.append((count - 1, 0))
        backward = [(target, source) for source, target in forward]
        low = lax.ppermute(
            lax.slice_in_dim(block, block.shape[dim] - width, None, axis=dim), axis, forward
        )
        high = lax.ppermute(lax.slice_in_dim(block, 0, width, axis=dim), axis, backward)
        block = jnp.concatenate([low, block, high], axis=dim)
    return block


def interface(padded, along):
    length = padded.shape[along]
    outer_low = lax.slice_in_dim(padded, 0, length - 3, axis=along)
    inner_low = lax.slice_in_dim(padded, 1, length - 2, axis=along)
    inner_high = lax.slice_in_dim(padded, 2, length - 1, axis=along)
    outer_high = lax.slice_in_dim(padded, 3, length, axis=along)
    return (7.0 * (inner_low + inner_high) - (outer_low + outer_high)) / 12.0


def cell_cosine(first_row, row_count, total_rows):
    index_rows = first_row + jnp.arange(row_count, dtype=jnp.int32)
    return jnp.sin(jnp.pi * (index_rows.astype(jnp.float32) + 0.5) / total_rows)


def face_cosine(first_row, row_count, total_rows):
    index_faces = first_row + jnp.arange(row_count + 1, dtype=jnp.int32)
    raw_values = jnp.sin(jnp.pi * index_faces.astype(jnp.float32) / total_rows)
    return jnp.where((index_faces == 0) | (index_faces == total_rows), 0.0, raw_values)


def local_basis(first_col, col_count, total_cols):
    positions = first_col + jnp.arange(col_count, dtype=jnp.int32)
    product_index = positions[:, None] * jnp.arange(KMAX, dtype=jnp.int32)[None, :] % total_cols
    phases = product_index.astype(jnp.float32) * (2.0 * jnp.pi / total_cols)
    return jnp.concatenate([jnp.cos(phases), jnp.sin(phases)], axis=1)


def mode_weights(cut_rows, total_cols):
    mode_index = jnp.arange(2 * KMAX, dtype=jnp.int32) % KMAX
    mode_scale = jnp.where(mode_index == 0, 1.0 / total_cols, 2.0 / total_cols).astype(jnp.float32)
    return jnp.where(mode_index[None, :] < cut_rows[:, None], mode_scale[None, :], 0.0)


def swap_halves(block, core_index):
    half = block.shape[0] // 2
    low, high = block[:half], block[half:]
    keep = jnp.where(core_index == 0, low, high)
    give = jnp.where(core_index == 0, high, low)
    return keep, lax.ppermute(give, "core", [(0, 1), (1, 0)])


def run_filter(row_values, cut_rows, first_col, total_cols):
    fields, levels, row_count, col_count = row_values.shape
    rings = lax.axis_size("ring")
    core_index = lax.axis_index("core")
    basis = local_basis(first_col, col_count, total_cols)
    flat = row_values.reshape(fields * levels * row_count, col_count)
    partial = jnp.dot(flat, basis, precision=lax.Precision.HIGHEST)
    keep, got = swap_halves(partial, core_index)
    chip_sum = (keep + got).reshape(rings, -1, 2 * KMAX)
    pieces = lax.all_to_all(chip_sum, "ring", 0, 0, tiled=True)
    ring_sum = jnp.sum(pieces, axis=0)
    reduced = ring_sum + lax.ppermute(ring_sum, "pair", [(0, 1), (1, 0)])
    spread = jnp.broadcast_to(reduced[None], (rings,) + reduced.shape)
    gathered = lax.all_to_all(spread, "ring", 0, 0, tiled=True).reshape(-1, 2 * KMAX)
    other = lax.ppermute(gathered, "core", [(0, 1), (1, 0)])
    low = jnp.where(core_index == 0, gathered, other)
    high = jnp.where(core_index == 0, other, gathered)
    coefficients = jnp.concatenate([low, high], axis=0).reshape(fields * levels, row_count, 2 * KMAX)
    weighted = coefficients * mode_weights(cut_rows, total_cols)[None]
    smooth = jnp.dot(weighted.reshape(-1, 2 * KMAX), basis.T, precision=lax.Precision.HIGHEST)
    return smooth.reshape(fields, levels, row_count, col_count)


def local(base_state, section_state, cutoff, filter_mask):
    fields, levels, row_count, col_count = section_state.shape
    lat_count = lax.axis_size("lat")
    lon_count = lax.axis_size(LON)
    lon_index = lax.axis_index(LON)
    band_index = lax.axis_index("lat")
    total_rows = row_count * lat_count
    total_cols = col_count * lon_count
    first_row = band_index * row_count
    flip_sign = jnp.where(jnp.arange(fields) < 2, -1.0, 1.0).astype(jnp.float32)[:, None, None]
    polar_edge = jnp.where(
        band_index == 0, section_state[:, :, 0, :], section_state[:, :, row_count - 1, :]
    )
    crossed = passed_along(polar_edge, LON, lon_count // 2) * flip_sign
    lat_padded = padded_2(section_state, (("lat", 2),), 2, False)
    south_row = jnp.where(band_index == 0, crossed, lat_padded[:, :, 1, :])
    north_row = jnp.where(band_index == lat_count - 1, crossed, lat_padded[:, :, row_count + 2, :])
    lat_padded = lat_padded.at[:, :, 1, :].set(south_row).at[:, :, row_count + 2, :].set(north_row)
    lon_padded = padded_2(section_state, ((LON, 3),), 2, True)
    face_cos = face_cosine(first_row, row_count, total_rows)
    cell_cos = cell_cosine(first_row, row_count, total_rows)
    lat_faces = interface(lat_padded, 2)
    lon_faces = interface(lon_padded, 3)
    north_flux = lat_faces[1][None] * lat_faces * face_cos[None, None, :, None]
    east_flux = lon_faces[0][None] * lon_faces
    tendency = (
        -(east_flux[..., 1:] - east_flux[..., :-1] + (north_flux[:, :, 1:] - north_flux[:, :, :-1]))
        / cell_cos[None, None, :, None]
    )
    own_mask = lax.dynamic_slice_in_dim(filter_mask, first_row, row_count)
    cut_rows = lax.dynamic_slice_in_dim(cutoff, first_row, row_count)
    smooth = run_filter(tendency, cut_rows, lon_index * col_count, total_cols)
    filtered = jnp.where(own_mask[None, None, :, None] == 1, smooth, tendency)
    return base_state + section_weight * filtered


def solution(mesh):
    rings = mesh.shape["lon"] // 4
    mesh = jax.sharding.Mesh(mesh.devices.reshape(mesh.shape["lat"], rings, 2, 2), ("lat",) + LON)
    placed = (P(None, None, "lat", LON), P(None, None, "lat", LON), P(), P())
    return jax.shard_map(
        local, mesh=mesh, in_specs=placed, out_specs=P(None, None, "lat", LON), check_vma=False
    )
```

```python
import jax
import jax.numpy as jnp
from jax import lax
from jax.sharding import PartitionSpec as P

KMAX = 64
LON = ("ring", "pair", "core")


section_weight = 0.4


def passed_along(block, axis, distance):
    devices = range(lax.axis_size(axis))
    route = [((i - distance) % len(devices), i) for i in devices]
    return lax.ppermute(block, axis, route)


def padded_2(block, sides, width, periodic):
    for axis, dim in sides:
        count = lax.axis_size(axis)
        forward = [(i, i + 1) for i in range(count - 1)]
        if periodic:
            forward.append((count - 1, 0))
        backward = [(target, source) for source, target in forward]
        low = lax.ppermute(
            lax.slice_in_dim(block, block.shape[dim] - width, None, axis=dim), axis, forward
        )
        high = lax.ppermute(lax.slice_in_dim(block, 0, width, axis=dim), axis, backward)
        block = jnp.concatenate([low, block, high], axis=dim)
    return block


def interface(padded, along):
    length = padded.shape[along]
    outer_low = lax.slice_in_dim(padded, 0, length - 3, axis=along)
    inner_low = lax.slice_in_dim(padded, 1, length - 2, axis=along)
    inner_high = lax.slice_in_dim(padded, 2, length - 1, axis=along)
    outer_high = lax.slice_in_dim(padded, 3, length, axis=along)
    return (7.0 * (inner_low + inner_high) - (outer_low + outer_high)) / 12.0


def cell_cosine(first_row, row_count, total_rows):
    index_rows = first_row + jnp.arange(row_count, dtype=jnp.int32)
    return jnp.sin(jnp.pi * (index_rows.astype(jnp.float32) + 0.5) / total_rows)


def face_cosine(first_row, row_count, total_rows):
    index_faces = first_row + jnp.arange(row_count + 1, dtype=jnp.int32)
    raw_values = jnp.sin(jnp.pi * index_faces.astype(jnp.float32) / total_rows)
    return jnp.where((index_faces == 0) | (index_faces == total_rows), 0.0, raw_values)


def local_basis(first_col, col_count, total_cols):
    positions = first_col + jnp.arange(col_count, dtype=jnp.int32)
    product_index = positions[:, None] * jnp.arange(KMAX, dtype=jnp.int32)[None, :] % total_cols
    phases = product_index.astype(jnp.float32) * (2.0 * jnp.pi / total_cols)
    return jnp.concatenate([jnp.cos(phases), jnp.sin(phases)], axis=1)


def mode_weights(cut_rows, total_cols):
    mode_index = jnp.arange(2 * KMAX, dtype=jnp.int32) % KMAX
    mode_scale = jnp.where(mode_index == 0, 1.0 / total_cols, 2.0 / total_cols).astype(jnp.float32)
    return jnp.where(mode_index[None, :] < cut_rows[:, None], mode_scale[None, :], 0.0)


def swap_halves(block, core_index):
    half = block.shape[0] // 2
    low, high = block[:half], block[half:]
    keep = jnp.where(core_index == 0, low, high)
    give = jnp.where(core_index == 0, high, low)
    return keep, lax.ppermute(give, "core", [(0, 1), (1, 0)])


def run_filter(row_values, cut_rows, first_col, total_cols):
    fields, levels, row_count, col_count = row_values.shape
    rings = lax.axis_size("ring")
    core_index = lax.axis_index("core")
    basis = local_basis(first_col, col_count, total_cols)
    flat = row_values.reshape(fields * levels * row_count, col_count)
    partial = jnp.dot(flat, basis, precision=lax.Precision.HIGHEST)
    keep, got = swap_halves(partial, core_index)
    chip_sum = (keep + got).reshape(rings, -1, 2 * KMAX)
    pieces = lax.all_to_all(chip_sum, "ring", 0, 0, tiled=True)
    ring_sum = jnp.sum(pieces, axis=0)
    reduced = ring_sum + lax.ppermute(ring_sum, "pair", [(0, 1), (1, 0)])
    spread = jnp.broadcast_to(reduced[None], (rings,) + reduced.shape)
    gathered = lax.all_to_all(spread, "ring", 0, 0, tiled=True).reshape(-1, 2 * KMAX)
    other = lax.ppermute(gathered, "core", [(0, 1), (1, 0)])
    low = jnp.where(core_index == 0, gathered, other)
    high = jnp.where(core_index == 0, other, gathered)
    coefficients = jnp.concatenate([low, high], axis=0).reshape(fields * levels, row_count, 2 * KMAX)
    weighted = coefficients * mode_weights(cut_rows, total_cols)[None]
    smooth = jnp.dot(weighted.reshape(-1, 2 * KMAX), basis.T, precision=lax.Precision.HIGHEST)
    return smooth.reshape(fields, levels, row_count, col_count)


def local(base_state, section_state, cutoff, filter_mask):
    fields, levels, row_count, col_count = section_state.shape
    lat_count = lax.axis_size("lat")
    lon_count = lax.axis_size(LON)
    lon_index = lax.axis_index(LON)
    band_index = lax.axis_index("lat")
    total_rows = row_count * lat_count
    total_cols = col_count * lon_count
    first_row = band_index * row_count
    flip_sign = jnp.where(jnp.arange(fields) < 2, -1.0, 1.0).astype(jnp.float32)[:, None, None]
    polar_edge = jnp.where(
        band_index == 0, section_state[:, :, 0, :], section_state[:, :, row_count - 1, :]
    )
    polar_pairs = [
        (band * lon_count + (i + lon_count // 2) % lon_count, band * lon_count + i)
        for band in (0, lat_count - 1)
        for i in range(lon_count)
    ]
    crossed = lax.ppermute(polar_edge, ("lat",) + LON, polar_pairs) * flip_sign
    lat_padded = padded_2(section_state, (("lat", 2),), 2, False)
    south_row = jnp.where(band_index == 0, crossed, lat_padded[:, :, 1, :])
    north_row = jnp.where(band_index == lat_count - 1, crossed, lat_padded[:, :, row_count + 2, :])
    lat_padded = lat_padded.at[:, :, 1, :].set(south_row).at[:, :, row_count + 2, :].set(north_row)
    lon_padded = padded_2(section_state, ((LON, 3),), 2, True)
    face_cos = face_cosine(first_row, row_count, total_rows)
    cell_cos = cell_cosine(first_row, row_count, total_rows)
    lat_faces = interface(lat_padded, 2)
    lon_faces = interface(lon_padded, 3)
    north_flux = lat_faces[1][None] * lat_faces * face_cos[None, None, :, None]
    east_flux = lon_faces[0][None] * lon_faces
    tendency = (
        -(east_flux[..., 1:] - east_flux[..., :-1] + (north_flux[:, :, 1:] - north_flux[:, :, :-1]))
        / cell_cos[None, None, :, None]
    )
    own_mask = lax.dynamic_slice_in_dim(filter_mask, first_row, row_count)
    cut_rows = lax.dynamic_slice_in_dim(cutoff, first_row, row_count)
    smooth = run_filter(tendency, cut_rows, lon_index * col_count, total_cols)
    filtered = jnp.where(own_mask[None, None, :, None] == 1, smooth, tendency)
    return base_state + section_weight * filtered


def solution(mesh):
    rings = mesh.shape["lon"] // 4
    mesh = jax.sharding.Mesh(mesh.devices.reshape(mesh.shape["lat"], rings, 2, 2), ("lat",) + LON)
    placed = (P(None, None, "lat", LON), P(None, None, "lat", LON), P(), P())
    return jax.shard_map(
        local, mesh=mesh, in_specs=placed, out_specs=P(None, None, "lat", LON), check_vma=False
    )
```

```python
import jax
import jax.numpy as jnp
from jax import lax
from jax.sharding import PartitionSpec as P

KMAX = 64
LON = ("ring", "pair", "core")


section_weight = 0.4


def passed_along(block, axis, distance):
    devices = range(lax.axis_size(axis))
    route = [((i - distance) % len(devices), i) for i in devices]
    return lax.ppermute(block, axis, route)


def padded_2(block, sides, width, periodic):
    for axis, dim in sides:
        count = lax.axis_size(axis)
        forward = [(i, i + 1) for i in range(count - 1)]
        if periodic:
            forward.append((count - 1, 0))
        backward = [(target, source) for source, target in forward]
        low = lax.ppermute(
            lax.slice_in_dim(block, block.shape[dim] - width, None, axis=dim), axis, forward
        )
        high = lax.ppermute(lax.slice_in_dim(block, 0, width, axis=dim), axis, backward)
        block = jnp.concatenate([low, block, high], axis=dim)
    return block


def interface(padded, along):
    length = padded.shape[along]
    outer_low = lax.slice_in_dim(padded, 0, length - 3, axis=along)
    inner_low = lax.slice_in_dim(padded, 1, length - 2, axis=along)
    inner_high = lax.slice_in_dim(padded, 2, length - 1, axis=along)
    outer_high = lax.slice_in_dim(padded, 3, length, axis=along)
    return (7.0 * (inner_low + inner_high) - (outer_low + outer_high)) / 12.0


def cell_cosine(first_row, row_count, total_rows):
    index_rows = first_row + jnp.arange(row_count, dtype=jnp.int32)
    return jnp.sin(jnp.pi * (index_rows.astype(jnp.float32) + 0.5) / total_rows)


def face_cosine(first_row, row_count, total_rows):
    index_faces = first_row + jnp.arange(row_count + 1, dtype=jnp.int32)
    raw_values = jnp.sin(jnp.pi * index_faces.astype(jnp.float32) / total_rows)
    return jnp.where((index_faces == 0) | (index_faces == total_rows), 0.0, raw_values)


def local_basis(first_col, col_count, total_cols):
    positions = first_col + jnp.arange(col_count, dtype=jnp.int32)
    product_index = positions[:, None] * jnp.arange(KMAX, dtype=jnp.int32)[None, :] % total_cols
    phases = product_index.astype(jnp.float32) * (2.0 * jnp.pi / total_cols)
    return jnp.concatenate([jnp.cos(phases), jnp.sin(phases)], axis=1)


def mode_weights(cut_rows, total_cols):
    mode_index = jnp.arange(2 * KMAX, dtype=jnp.int32) % KMAX
    mode_scale = jnp.where(mode_index == 0, 1.0 / total_cols, 2.0 / total_cols).astype(jnp.float32)
    return jnp.where(mode_index[None, :] < cut_rows[:, None], mode_scale[None, :], 0.0)


def swap_halves(block, core_index):
    half = block.shape[0] // 2
    low, high = block[:half], block[half:]
    keep = jnp.where(core_index == 0, low, high)
    give = jnp.where(core_index == 0, high, low)
    return keep, lax.ppermute(give, "core", [(0, 1), (1, 0)])


def run_filter(row_values, cut_rows, first_col, total_cols):
    fields, levels, row_count, col_count = row_values.shape
    rings = lax.axis_size("ring")
    core_index = lax.axis_index("core")
    basis = local_basis(first_col, col_count, total_cols)
    flat = row_values.reshape(fields * levels * row_count, col_count)
    partial = jnp.dot(flat, basis, precision=lax.Precision.HIGHEST)
    keep, got = swap_halves(partial, core_index)
    chip_sum = (keep + got).reshape(rings, -1, 2 * KMAX)
    pieces = lax.all_to_all(chip_sum, "ring", 0, 0, tiled=True)
    ring_sum = jnp.sum(pieces, axis=0)
    reduced = ring_sum + lax.ppermute(ring_sum, "pair", [(0, 1), (1, 0)])
    spread = jnp.broadcast_to(reduced[None], (rings,) + reduced.shape)
    gathered = lax.all_to_all(spread, "ring", 0, 0, tiled=True).reshape(-1, 2 * KMAX)
    other = lax.ppermute(gathered, "core", [(0, 1), (1, 0)])
    low = jnp.where(core_index == 0, gathered, other)
    high = jnp.where(core_index == 0, other, gathered)
    coefficients = jnp.concatenate([low, high], axis=0).reshape(fields * levels, row_count, 2 * KMAX)
    weighted = coefficients * mode_weights(cut_rows, total_cols)[None]
    smooth = jnp.dot(weighted.reshape(-1, 2 * KMAX), basis.T, precision=lax.Precision.HIGHEST)
    return smooth.reshape(fields, levels, row_count, col_count)


def ring_pairs(lat_count, lon_count, upward):
    half = lon_count // 2
    pairs = []
    for i in range(lat_count):
        for j in range(lon_count):
            north_going = (j < half) == upward
            if north_going:
                target = (i + 1, j) if i < lat_count - 1 else (i, (j + half) % lon_count)
            else:
                target = (i - 1, j) if i > 0 else (i, (j + half) % lon_count)
            pairs.append((i * lon_count + j, target[0] * lon_count + target[1]))
    return pairs


def ring_padded(block, flip_sign, band_index, lon_index, lat_count, lon_count):
    first = block[:, :, :2]
    last = block[:, :, -2:]
    far_half = lon_index >= lon_count // 2
    axes = ("lat",) + LON
    up = lax.ppermute(jnp.where(far_half, first, last), axes, ring_pairs(lat_count, lon_count, True))
    down = lax.ppermute(jnp.where(far_half, last, first), axes, ring_pairs(lat_count, lon_count, False))
    south = jnp.where(far_half, down, up)
    north = jnp.where(far_half, up, down)
    zero = jnp.zeros_like(south[:, :, :1])
    south_pole = jnp.concatenate([zero, flip_sign * south[:, :, :1]], axis=2)
    north_pole = jnp.concatenate([flip_sign * north[:, :, 1:], zero], axis=2)
    south = jnp.where(band_index == 0, south_pole, south)
    north = jnp.where(band_index == lat_count - 1, north_pole, north)
    return jnp.concatenate([south, block, north], axis=2)


def local(base_state, section_state, cutoff, filter_mask):
    fields, levels, row_count, col_count = section_state.shape
    lat_count = lax.axis_size("lat")
    lon_count = lax.axis_size(LON)
    lon_index = lax.axis_index(LON)
    band_index = lax.axis_index("lat")
    total_rows = row_count * lat_count
    total_cols = col_count * lon_count
    first_row = band_index * row_count
    flip_sign = jnp.where(jnp.arange(fields) < 2, -1.0, 1.0).astype(jnp.float32)[:, None, None, None]
    lat_padded = ring_padded(section_state, flip_sign, band_index, lon_index, lat_count, lon_count)
    lon_padded = padded_2(section_state, ((LON, 3),), 2, True)
    face_cos = face_cosine(first_row, row_count, total_rows)
    cell_cos = cell_cosine(first_row, row_count, total_rows)
    lat_faces = interface(lat_padded, 2)
    lon_faces = interface(lon_padded, 3)
    north_flux = lat_faces[1][None] * lat_faces * face_cos[None, None, :, None]
    east_flux = lon_faces[0][None] * lon_faces
    tendency = (
        -(east_flux[..., 1:] - east_flux[..., :-1] + (north_flux[:, :, 1:] - north_flux[:, :, :-1]))
        / cell_cos[None, None, :, None]
    )
    own_mask = lax.dynamic_slice_in_dim(filter_mask, first_row, row_count)
    cut_rows = lax.dynamic_slice_in_dim(cutoff, first_row, row_count)
    smooth = run_filter(tendency, cut_rows, lon_index * col_count, total_cols)
    filtered = jnp.where(own_mask[None, None, :, None] == 1, smooth, tendency)
    return base_state + section_weight * filtered


def solution(mesh):
    rings = mesh.shape["lon"] // 4
    mesh = jax.sharding.Mesh(mesh.devices.reshape(mesh.shape["lat"], rings, 2, 2), ("lat",) + LON)
    placed = (P(None, None, "lat", LON), P(None, None, "lat", LON), P(), P())
    return jax.shard_map(
        local, mesh=mesh, in_specs=placed, out_specs=P(None, None, "lat", LON), check_vma=False
    )
```

```python
import jax
import jax.numpy as jnp
from jax import lax
from jax.sharding import PartitionSpec as P

KMAX = 64
LON = ("ring", "pair", "core")


section_weight = 0.4


def passed_along(block, axis, distance):
    devices = range(lax.axis_size(axis))
    route = [((i - distance) % len(devices), i) for i in devices]
    return lax.ppermute(block, axis, route)


def padded_2(block, sides, width, periodic):
    for axis, dim in sides:
        count = lax.axis_size(axis)
        forward = [(i, i + 1) for i in range(count - 1)]
        if periodic:
            forward.append((count - 1, 0))
        backward = [(target, source) for source, target in forward]
        low = lax.ppermute(
            lax.slice_in_dim(block, block.shape[dim] - width, None, axis=dim), axis, forward
        )
        high = lax.ppermute(lax.slice_in_dim(block, 0, width, axis=dim), axis, backward)
        block = jnp.concatenate([low, block, high], axis=dim)
    return block


def interface(padded, along):
    length = padded.shape[along]
    outer_low = lax.slice_in_dim(padded, 0, length - 3, axis=along)
    inner_low = lax.slice_in_dim(padded, 1, length - 2, axis=along)
    inner_high = lax.slice_in_dim(padded, 2, length - 1, axis=along)
    outer_high = lax.slice_in_dim(padded, 3, length, axis=along)
    return (7.0 * (inner_low + inner_high) - (outer_low + outer_high)) / 12.0


def cell_cosine(first_row, row_count, total_rows):
    index_rows = first_row + jnp.arange(row_count, dtype=jnp.int32)
    return jnp.sin(jnp.pi * (index_rows.astype(jnp.float32) + 0.5) / total_rows)


def face_cosine(first_row, row_count, total_rows):
    index_faces = first_row + jnp.arange(row_count + 1, dtype=jnp.int32)
    raw_values = jnp.sin(jnp.pi * index_faces.astype(jnp.float32) / total_rows)
    return jnp.where((index_faces == 0) | (index_faces == total_rows), 0.0, raw_values)


def local_basis(first_col, col_count, total_cols):
    positions = first_col + jnp.arange(col_count, dtype=jnp.int32)
    product_index = positions[:, None] * jnp.arange(KMAX, dtype=jnp.int32)[None, :] % total_cols
    phases = product_index.astype(jnp.float32) * (2.0 * jnp.pi / total_cols)
    return jnp.concatenate([jnp.cos(phases), jnp.sin(phases)], axis=1)


def mode_weights(cut_rows, total_cols):
    mode_index = jnp.arange(2 * KMAX, dtype=jnp.int32) % KMAX
    mode_scale = jnp.where(mode_index == 0, 1.0 / total_cols, 2.0 / total_cols).astype(jnp.float32)
    return jnp.where(mode_index[None, :] < cut_rows[:, None], mode_scale[None, :], 0.0)


def swap_halves(block, core_index):
    half = block.shape[0] // 2
    low, high = block[:half], block[half:]
    keep = jnp.where(core_index == 0, low, high)
    give = jnp.where(core_index == 0, high, low)
    return keep, lax.ppermute(give, "core", [(0, 1), (1, 0)])


def run_filter(row_values, cut_rows, first_col, total_cols):
    fields, levels, row_count, col_count = row_values.shape
    rings = lax.axis_size("ring")
    core_index = lax.axis_index("core")
    basis = local_basis(first_col, col_count, total_cols)
    flat = row_values.reshape(fields * levels * row_count, col_count)
    partial = jnp.dot(flat, basis, precision=lax.Precision.HIGHEST)
    keep, got = swap_halves(partial, core_index)
    chip_sum = (keep + got).reshape(rings, -1, 2 * KMAX)
    pieces = lax.all_to_all(chip_sum, "ring", 0, 0, tiled=True)
    ring_sum = jnp.sum(pieces, axis=0)
    reduced = ring_sum + lax.ppermute(ring_sum, "pair", [(0, 1), (1, 0)])
    spread = jnp.broadcast_to(reduced[None], (rings,) + reduced.shape)
    gathered = lax.all_to_all(spread, "ring", 0, 0, tiled=True).reshape(-1, 2 * KMAX)
    other = lax.ppermute(gathered, "core", [(0, 1), (1, 0)])
    low = jnp.where(core_index == 0, gathered, other)
    high = jnp.where(core_index == 0, other, gathered)
    coefficients = jnp.concatenate([low, high], axis=0).reshape(fields * levels, row_count, 2 * KMAX)
    weighted = coefficients * mode_weights(cut_rows, total_cols)[None]
    smooth = jnp.dot(weighted.reshape(-1, 2 * KMAX), basis.T, precision=lax.Precision.HIGHEST)
    return smooth.reshape(fields, levels, row_count, col_count)


def ring_pairs(lat_count, lon_count, upward):
    half = lon_count // 2
    pairs = []
    for i in range(lat_count):
        for j in range(lon_count):
            north_going = (j < half) == upward
            if north_going:
                target = (i + 1, j) if i < lat_count - 1 else (i, (j + half) % lon_count)
            else:
                target = (i - 1, j) if i > 0 else (i, (j + half) % lon_count)
            pairs.append((i * lon_count + j, target[0] * lon_count + target[1]))
    return pairs


def ring_padded(block, flip_sign, band_index, lon_index, lat_count, lon_count):
    first = block[:, :, :2]
    last = block[:, :, -2:]
    far_half = lon_index >= lon_count // 2
    axes = ("lat",) + LON
    up = lax.ppermute(jnp.where(far_half, first, last), axes, ring_pairs(lat_count, lon_count, True))
    down = lax.ppermute(jnp.where(far_half, last, first), axes, ring_pairs(lat_count, lon_count, False))
    south = jnp.where(far_half, down, up)
    north = jnp.where(far_half, up, down)
    zero = jnp.zeros_like(south[:, :, :1])
    south_pole = jnp.concatenate([zero, flip_sign * south[:, :, :1]], axis=2)
    north_pole = jnp.concatenate([flip_sign * north[:, :, 1:], zero], axis=2)
    south = jnp.where(band_index == 0, south_pole, south)
    north = jnp.where(band_index == lat_count - 1, north_pole, north)
    return jnp.concatenate([south, block, north], axis=2)


def local(base_state, section_state, cutoff, filter_mask):
    fields, levels, row_count, col_count = section_state.shape
    lat_count = lax.axis_size("lat")
    lon_count = lax.axis_size(LON)
    lon_index = lax.axis_index(LON)
    band_index = lax.axis_index("lat")
    total_rows = row_count * lat_count
    total_cols = col_count * lon_count
    first_row = band_index * row_count
    flip_sign = jnp.where(jnp.arange(fields) < 2, -1.0, 1.0).astype(jnp.float32)[:, None, None, None]
    lat_padded = ring_padded(section_state, flip_sign, band_index, lon_index, lat_count, lon_count)
    lon_padded = padded_2(section_state, ((LON, 3),), 2, True)
    face_cos = face_cosine(first_row, row_count, total_rows)
    cell_cos = cell_cosine(first_row, row_count, total_rows)
    lat_faces = interface(lat_padded, 2)
    lon_faces = interface(lon_padded, 3)
    north_flux = lat_faces[1][None] * lat_faces * face_cos[None, None, :, None]
    east_flux = lon_faces[0][None] * lon_faces
    tendency = (
        -(east_flux[..., 1:] - east_flux[..., :-1] + (north_flux[:, :, 1:] - north_flux[:, :, :-1]))
        / cell_cos[None, None, :, None]
    )
    own_mask = lax.dynamic_slice_in_dim(filter_mask, first_row, row_count)
    cut_rows = lax.dynamic_slice_in_dim(cutoff, first_row, row_count)
    half_fields = fields // 2
    smooth = jnp.concatenate(
        [
            run_filter(tendency[:half_fields], cut_rows, lon_index * col_count, total_cols),
            run_filter(tendency[half_fields:], cut_rows, lon_index * col_count, total_cols),
        ],
        axis=0,
    )
    filtered = jnp.where(own_mask[None, None, :, None] == 1, smooth, tendency)
    return base_state + section_weight * filtered


def solution(mesh):
    rings = mesh.shape["lon"] // 4
    mesh = jax.sharding.Mesh(mesh.devices.reshape(mesh.shape["lat"], rings, 2, 2), ("lat",) + LON)
    placed = (P(None, None, "lat", LON), P(None, None, "lat", LON), P(), P())
    return jax.shard_map(
        local, mesh=mesh, in_specs=placed, out_specs=P(None, None, "lat", LON), check_vma=False
    )
```

```python
import jax
import jax.numpy as jnp
from jax import lax
from jax.sharding import PartitionSpec as P

KMAX = 64
LON = ("ring", "pair", "core")


section_weight = 0.4


def passed_along(block, axis, distance):
    devices = range(lax.axis_size(axis))
    route = [((i - distance) % len(devices), i) for i in devices]
    return lax.ppermute(block, axis, route)


def padded_2(block, sides, width, periodic):
    for axis, dim in sides:
        count = lax.axis_size(axis)
        forward = [(i, i + 1) for i in range(count - 1)]
        if periodic:
            forward.append((count - 1, 0))
        backward = [(target, source) for source, target in forward]
        low = lax.ppermute(
            lax.slice_in_dim(block, block.shape[dim] - width, None, axis=dim), axis, forward
        )
        high = lax.ppermute(lax.slice_in_dim(block, 0, width, axis=dim), axis, backward)
        block = jnp.concatenate([low, block, high], axis=dim)
    return block


def interface(padded, along):
    length = padded.shape[along]
    outer_low = lax.slice_in_dim(padded, 0, length - 3, axis=along)
    inner_low = lax.slice_in_dim(padded, 1, length - 2, axis=along)
    inner_high = lax.slice_in_dim(padded, 2, length - 1, axis=along)
    outer_high = lax.slice_in_dim(padded, 3, length, axis=along)
    return (7.0 * (inner_low + inner_high) - (outer_low + outer_high)) / 12.0


def cell_cosine(first_row, row_count, total_rows):
    index_rows = first_row + jnp.arange(row_count, dtype=jnp.int32)
    return jnp.sin(jnp.pi * (index_rows.astype(jnp.float32) + 0.5) / total_rows)


def face_cosine(first_row, row_count, total_rows):
    index_faces = first_row + jnp.arange(row_count + 1, dtype=jnp.int32)
    raw_values = jnp.sin(jnp.pi * index_faces.astype(jnp.float32) / total_rows)
    return jnp.where((index_faces == 0) | (index_faces == total_rows), 0.0, raw_values)


def local_basis(first_col, col_count, total_cols):
    positions = first_col + jnp.arange(col_count, dtype=jnp.int32)
    product_index = positions[:, None] * jnp.arange(KMAX, dtype=jnp.int32)[None, :] % total_cols
    phases = product_index.astype(jnp.float32) * (2.0 * jnp.pi / total_cols)
    return jnp.concatenate([jnp.cos(phases), jnp.sin(phases)], axis=1)


def mode_weights(cut_rows, total_cols):
    mode_index = jnp.arange(2 * KMAX, dtype=jnp.int32) % KMAX
    mode_scale = jnp.where(mode_index == 0, 1.0 / total_cols, 2.0 / total_cols).astype(jnp.float32)
    return jnp.where(mode_index[None, :] < cut_rows[:, None], mode_scale[None, :], 0.0)


def swap_halves(block, core_index):
    half = block.shape[0] // 2
    low, high = block[:half], block[half:]
    keep = jnp.where(core_index == 0, low, high)
    give = jnp.where(core_index == 0, high, low)
    return keep, lax.ppermute(give, "core", [(0, 1), (1, 0)])


def run_filter(row_values, cut_rows, first_col, total_cols):
    fields, levels, row_count, col_count = row_values.shape
    rings = lax.axis_size("ring")
    core_index = lax.axis_index("core")
    basis = local_basis(first_col, col_count, total_cols)
    flat = row_values.reshape(fields * levels * row_count, col_count)
    partial = jnp.dot(flat, basis, precision=lax.Precision.HIGHEST)
    keep, got = swap_halves(partial, core_index)
    chip_sum = (keep + got).reshape(rings, -1, 2 * KMAX)
    pieces = lax.all_to_all(chip_sum, "ring", 0, 0, tiled=True)
    ring_sum = jnp.sum(pieces, axis=0)
    reduced = ring_sum + lax.ppermute(ring_sum, "pair", [(0, 1), (1, 0)])
    spread = jnp.broadcast_to(reduced[None], (rings,) + reduced.shape)
    gathered = lax.all_to_all(spread, "ring", 0, 0, tiled=True).reshape(-1, 2 * KMAX)
    other = lax.ppermute(gathered, "core", [(0, 1), (1, 0)])
    low = jnp.where(core_index == 0, gathered, other)
    high = jnp.where(core_index == 0, other, gathered)
    coefficients = jnp.concatenate([low, high], axis=0).reshape(fields * levels, row_count, 2 * KMAX)
    weighted = coefficients * mode_weights(cut_rows, total_cols)[None]
    smooth = jnp.dot(weighted.reshape(-1, 2 * KMAX), basis.T, precision=lax.Precision.HIGHEST)
    return smooth.reshape(fields, levels, row_count, col_count)


def ring_pairs(lat_count, lon_count, upward):
    half = lon_count // 2
    pairs = []
    for i in range(lat_count):
        for j in range(lon_count):
            north_going = (j < half) == upward
            if north_going:
                target = (i + 1, j) if i < lat_count - 1 else (i, (j + half) % lon_count)
            else:
                target = (i - 1, j) if i > 0 else (i, (j + half) % lon_count)
            pairs.append((i * lon_count + j, target[0] * lon_count + target[1]))
    return pairs


def ring_padded(block, flip_sign, band_index, lon_index, lat_count, lon_count):
    first = block[:, :, :2]
    last = block[:, :, -2:]
    far_half = lon_index >= lon_count // 2
    axes = ("lat",) + LON
    up = lax.ppermute(jnp.where(far_half, first, last), axes, ring_pairs(lat_count, lon_count, True))
    down = lax.ppermute(jnp.where(far_half, last, first), axes, ring_pairs(lat_count, lon_count, False))
    south = jnp.where(far_half, down, up)
    north = jnp.where(far_half, up, down)
    zero = jnp.zeros_like(south[:, :, :1])
    south_pole = jnp.concatenate([zero, flip_sign * south[:, :, :1]], axis=2)
    north_pole = jnp.concatenate([flip_sign * north[:, :, 1:], zero], axis=2)
    south = jnp.where(band_index == 0, south_pole, south)
    north = jnp.where(band_index == lat_count - 1, north_pole, north)
    return jnp.concatenate([south, block, north], axis=2)


def lon_halos(block, lon_index, lon_count):
    first = block[..., :2]
    last = block[..., -2:]
    odd = lon_index % 2 == 1
    across = [(j, (j + 1) % lon_count if j % 2 else (j - 1) % lon_count) for j in range(lon_count)]
    far = lax.ppermute(jnp.where(odd, last, first), LON, across)
    near = lax.ppermute(jnp.where(odd, first, last), LON, [(j, j ^ 1) for j in range(lon_count)])
    west = jnp.where(odd, near, far)
    east = jnp.where(odd, far, near)
    return jnp.concatenate([west, block, east], axis=3)


def local(base_state, section_state, cutoff, filter_mask):
    fields, levels, row_count, col_count = section_state.shape
    lat_count = lax.axis_size("lat")
    lon_count = lax.axis_size(LON)
    lon_index = lax.axis_index(LON)
    band_index = lax.axis_index("lat")
    total_rows = row_count * lat_count
    total_cols = col_count * lon_count
    first_row = band_index * row_count
    flip_sign = jnp.where(jnp.arange(fields) < 2, -1.0, 1.0).astype(jnp.float32)[:, None, None, None]
    lat_padded = ring_padded(section_state, flip_sign, band_index, lon_index, lat_count, lon_count)
    lon_padded = lon_halos(section_state, lon_index, lon_count)
    face_cos = face_cosine(first_row, row_count, total_rows)
    cell_cos = cell_cosine(first_row, row_count, total_rows)
    lat_faces = interface(lat_padded, 2)
    lon_faces = interface(lon_padded, 3)
    north_flux = lat_faces[1][None] * lat_faces * face_cos[None, None, :, None]
    east_flux = lon_faces[0][None] * lon_faces
    tendency = (
        -(east_flux[..., 1:] - east_flux[..., :-1] + (north_flux[:, :, 1:] - north_flux[:, :, :-1]))
        / cell_cos[None, None, :, None]
    )
    own_mask = lax.dynamic_slice_in_dim(filter_mask, first_row, row_count)
    cut_rows = lax.dynamic_slice_in_dim(cutoff, first_row, row_count)
    smooth = run_filter(tendency, cut_rows, lon_index * col_count, total_cols)
    filtered = jnp.where(own_mask[None, None, :, None] == 1, smooth, tendency)
    return base_state + section_weight * filtered


def solution(mesh):
    rings = mesh.shape["lon"] // 4
    mesh = jax.sharding.Mesh(mesh.devices.reshape(mesh.shape["lat"], rings, 2, 2), ("lat",) + LON)
    placed = (P(None, None, "lat", LON), P(None, None, "lat", LON), P(), P())
    return jax.shard_map(
        local, mesh=mesh, in_specs=placed, out_specs=P(None, None, "lat", LON), check_vma=False
    )
```

```python
import jax
import jax.numpy as jnp
from jax import lax
from jax.sharding import PartitionSpec as P

KMAX = 64
LON = ("ring", "pair", "core")


section_weight = 0.4


def passed_along(block, axis, distance):
    devices = range(lax.axis_size(axis))
    route = [((i - distance) % len(devices), i) for i in devices]
    return lax.ppermute(block, axis, route)


def padded_2(block, sides, width, periodic):
    for axis, dim in sides:
        count = lax.axis_size(axis)
        forward = [(i, i + 1) for i in range(count - 1)]
        if periodic:
            forward.append((count - 1, 0))
        backward = [(target, source) for source, target in forward]
        low = lax.ppermute(
            lax.slice_in_dim(block, block.shape[dim] - width, None, axis=dim), axis, forward
        )
        high = lax.ppermute(lax.slice_in_dim(block, 0, width, axis=dim), axis, backward)
        block = jnp.concatenate([low, block, high], axis=dim)
    return block


def interface(padded, along):
    length = padded.shape[along]
    outer_low = lax.slice_in_dim(padded, 0, length - 3, axis=along)
    inner_low = lax.slice_in_dim(padded, 1, length - 2, axis=along)
    inner_high = lax.slice_in_dim(padded, 2, length - 1, axis=along)
    outer_high = lax.slice_in_dim(padded, 3, length, axis=along)
    return (7.0 * (inner_low + inner_high) - (outer_low + outer_high)) / 12.0


def cell_cosine(first_row, row_count, total_rows):
    index_rows = first_row + jnp.arange(row_count, dtype=jnp.int32)
    return jnp.sin(jnp.pi * (index_rows.astype(jnp.float32) + 0.5) / total_rows)


def face_cosine(first_row, row_count, total_rows):
    index_faces = first_row + jnp.arange(row_count + 1, dtype=jnp.int32)
    raw_values = jnp.sin(jnp.pi * index_faces.astype(jnp.float32) / total_rows)
    return jnp.where((index_faces == 0) | (index_faces == total_rows), 0.0, raw_values)


def local_basis(first_col, col_count, total_cols):
    positions = first_col + jnp.arange(col_count, dtype=jnp.int32)
    product_index = positions[:, None] * jnp.arange(KMAX, dtype=jnp.int32)[None, :] % total_cols
    phases = product_index.astype(jnp.float32) * (2.0 * jnp.pi / total_cols)
    return jnp.concatenate([jnp.cos(phases), jnp.sin(phases)], axis=1)


def mode_weights(cut_rows, total_cols):
    mode_index = jnp.arange(2 * KMAX, dtype=jnp.int32) % KMAX
    mode_scale = jnp.where(mode_index == 0, 1.0 / total_cols, 2.0 / total_cols).astype(jnp.float32)
    return jnp.where(mode_index[None, :] < cut_rows[:, None], mode_scale[None, :], 0.0)


def swap_halves(block, core_index):
    half = block.shape[0] // 2
    low, high = block[:half], block[half:]
    keep = jnp.where(core_index == 0, low, high)
    give = jnp.where(core_index == 0, high, low)
    return keep, lax.ppermute(give, "core", [(0, 1), (1, 0)])


def run_filter(row_values, cut_rows, own_mask, first_col, total_cols):
    fields, levels, row_count, col_count = row_values.shape
    rings = lax.axis_size("ring")
    core_index = lax.axis_index("core")
    basis = local_basis(first_col, col_count, total_cols)
    flat = row_values.reshape(fields * levels * row_count, col_count)
    partial = jnp.dot(flat, basis, precision=lax.Precision.HIGHEST)
    keep, got = swap_halves(partial, core_index)
    chip_sum = (keep + got).reshape(rings, -1, 2 * KMAX)
    pieces = lax.all_to_all(chip_sum, "ring", 0, 0, tiled=True)
    ring_sum = jnp.sum(pieces, axis=0)
    reduced = ring_sum + lax.ppermute(ring_sum, "pair", [(0, 1), (1, 0)])
    chunk = reduced.shape[0]
    first_flat = core_index * (rings * chunk) + lax.axis_index("ring") * chunk
    chunk_cuts = jnp.take(cut_rows, (first_flat + jnp.arange(chunk, dtype=jnp.int32)) % row_count)
    weights = mode_weights(chunk_cuts, total_cols)
    weighted, own_mask = lax.optimization_barrier((reduced * weights, own_mask))
    spread = jnp.broadcast_to(weighted[None], (rings,) + weighted.shape)
    gathered = lax.all_to_all(spread, "ring", 0, 0, tiled=True).reshape(-1, 2 * KMAX)
    other = lax.ppermute(gathered, "core", [(0, 1), (1, 0)])
    low = jnp.where(core_index == 0, gathered, other)
    high = jnp.where(core_index == 0, other, gathered)
    coefficients = jnp.concatenate([low, high], axis=0)
    smooth = jnp.dot(coefficients, basis.T, precision=lax.Precision.HIGHEST)
    return smooth.reshape(fields, levels, row_count, col_count), own_mask


def ring_pairs(lat_count, lon_count, upward):
    half = lon_count // 2
    pairs = []
    for i in range(lat_count):
        for j in range(lon_count):
            north_going = (j < half) == upward
            if north_going:
                target = (i + 1, j) if i < lat_count - 1 else (i, (j + half) % lon_count)
            else:
                target = (i - 1, j) if i > 0 else (i, (j + half) % lon_count)
            pairs.append((i * lon_count + j, target[0] * lon_count + target[1]))
    return pairs


def ring_padded(block, flip_sign, band_index, lon_index, lat_count, lon_count):
    first = block[:, :, :2]
    last = block[:, :, -2:]
    far_half = lon_index >= lon_count // 2
    axes = ("lat",) + LON
    up = lax.ppermute(jnp.where(far_half, first, last), axes, ring_pairs(lat_count, lon_count, True))
    down = lax.ppermute(jnp.where(far_half, last, first), axes, ring_pairs(lat_count, lon_count, False))
    south = jnp.where(far_half, down, up)
    north = jnp.where(far_half, up, down)
    zero = jnp.zeros_like(south[:, :, :1])
    south_pole = jnp.concatenate([zero, flip_sign * south[:, :, :1]], axis=2)
    north_pole = jnp.concatenate([flip_sign * north[:, :, 1:], zero], axis=2)
    south = jnp.where(band_index == 0, south_pole, south)
    north = jnp.where(band_index == lat_count - 1, north_pole, north)
    return jnp.concatenate([south, block, north], axis=2)


def lon_halos(block, lon_index, lon_count):
    first = block[..., :2]
    last = block[..., -2:]
    odd = lon_index % 2 == 1
    across = [(j, (j + 1) % lon_count if j % 2 else (j - 1) % lon_count) for j in range(lon_count)]
    far = lax.ppermute(jnp.where(odd, last, first), LON, across)
    near = lax.ppermute(jnp.where(odd, first, last), LON, [(j, j ^ 1) for j in range(lon_count)])
    west = jnp.where(odd, near, far)
    east = jnp.where(odd, far, near)
    return jnp.concatenate([west, block, east], axis=3)


def local(base_state, section_state, cutoff, filter_mask):
    fields, levels, row_count, col_count = section_state.shape
    lat_count = lax.axis_size("lat")
    lon_count = lax.axis_size(LON)
    lon_index = lax.axis_index(LON)
    band_index = lax.axis_index("lat")
    total_rows = row_count * lat_count
    total_cols = col_count * lon_count
    first_row = band_index * row_count
    flip_sign = jnp.where(jnp.arange(fields) < 2, -1.0, 1.0).astype(jnp.float32)[:, None, None, None]
    lat_padded = ring_padded(section_state, flip_sign, band_index, lon_index, lat_count, lon_count)
    lon_padded = lon_halos(section_state, lon_index, lon_count)
    face_cos = face_cosine(first_row, row_count, total_rows)
    cell_cos = cell_cosine(first_row, row_count, total_rows)
    lat_faces = interface(lat_padded, 2)
    lon_faces = interface(lon_padded, 3)
    north_flux = lat_faces[1][None] * lat_faces * face_cos[None, None, :, None]
    east_flux = lon_faces[0][None] * lon_faces
    tendency = (
        -(east_flux[..., 1:] - east_flux[..., :-1] + (north_flux[:, :, 1:] - north_flux[:, :, :-1]))
        / cell_cos[None, None, :, None]
    )
    own_mask = lax.dynamic_slice_in_dim(filter_mask, first_row, row_count)
    cut_rows = lax.dynamic_slice_in_dim(cutoff, first_row, row_count)
    smooth, own_mask = run_filter(tendency, cut_rows, own_mask, lon_index * col_count, total_cols)
    filtered = jnp.where(own_mask[None, None, :, None] == 1, smooth, tendency)
    return base_state + section_weight * filtered


def solution(mesh):
    rings = mesh.shape["lon"] // 4
    mesh = jax.sharding.Mesh(mesh.devices.reshape(mesh.shape["lat"], rings, 2, 2), ("lat",) + LON)
    placed = (P(None, None, "lat", LON), P(None, None, "lat", LON), P(), P())
    return jax.shard_map(
        local, mesh=mesh, in_specs=placed, out_specs=P(None, None, "lat", LON), check_vma=False
    )
```

```python
import jax
import jax.numpy as jnp
from jax import lax
from jax.sharding import PartitionSpec as P

KMAX = 64
LON = ("ring", "pair", "core")


section_weight = 0.4


def passed_along(block, axis, distance):
    devices = range(lax.axis_size(axis))
    route = [((i - distance) % len(devices), i) for i in devices]
    return lax.ppermute(block, axis, route)


def padded_2(block, sides, width, periodic):
    for axis, dim in sides:
        count = lax.axis_size(axis)
        forward = [(i, i + 1) for i in range(count - 1)]
        if periodic:
            forward.append((count - 1, 0))
        backward = [(target, source) for source, target in forward]
        low = lax.ppermute(
            lax.slice_in_dim(block, block.shape[dim] - width, None, axis=dim), axis, forward
        )
        high = lax.ppermute(lax.slice_in_dim(block, 0, width, axis=dim), axis, backward)
        block = jnp.concatenate([low, block, high], axis=dim)
    return block


def interface(padded, along):
    length = padded.shape[along]
    outer_low = lax.slice_in_dim(padded, 0, length - 3, axis=along)
    inner_low = lax.slice_in_dim(padded, 1, length - 2, axis=along)
    inner_high = lax.slice_in_dim(padded, 2, length - 1, axis=along)
    outer_high = lax.slice_in_dim(padded, 3, length, axis=along)
    return (7.0 * (inner_low + inner_high) - (outer_low + outer_high)) / 12.0


def cell_cosine(first_row, row_count, total_rows):
    index_rows = first_row + jnp.arange(row_count, dtype=jnp.int32)
    return jnp.sin(jnp.pi * (index_rows.astype(jnp.float32) + 0.5) / total_rows)


def face_cosine(first_row, row_count, total_rows):
    index_faces = first_row + jnp.arange(row_count + 1, dtype=jnp.int32)
    raw_values = jnp.sin(jnp.pi * index_faces.astype(jnp.float32) / total_rows)
    return jnp.where((index_faces == 0) | (index_faces == total_rows), 0.0, raw_values)


def local_basis(first_col, col_count, total_cols):
    positions = first_col + jnp.arange(col_count, dtype=jnp.int32)
    product_index = positions[:, None] * jnp.arange(KMAX, dtype=jnp.int32)[None, :] % total_cols
    phases = product_index.astype(jnp.float32) * (2.0 * jnp.pi / total_cols)
    return jnp.concatenate([jnp.cos(phases), jnp.sin(phases)], axis=1)


def mode_weights(cut_rows, total_cols):
    mode_index = jnp.arange(2 * KMAX, dtype=jnp.int32) % KMAX
    mode_scale = jnp.where(mode_index == 0, 1.0 / total_cols, 2.0 / total_cols).astype(jnp.float32)
    return jnp.where(mode_index[None, :] < cut_rows[:, None], mode_scale[None, :], 0.0)


def swap_halves(block, core_index):
    half = block.shape[0] // 2
    low, high = block[:half], block[half:]
    keep = jnp.where(core_index == 0, low, high)
    give = jnp.where(core_index == 0, high, low)
    return keep, lax.ppermute(give, "core", [(0, 1), (1, 0)])


def run_filter(level_values, cut_rows, first_col, total_cols):
    fields, row_count, col_count = level_values.shape
    rings = lax.axis_size("ring")
    basis = local_basis(first_col, col_count, total_cols)
    chip_sum = jnp.dot(level_values.reshape(-1, col_count), basis, precision=lax.Precision.HIGHEST)
    pieces = lax.all_to_all(chip_sum.reshape(rings, -1, 2 * KMAX), "ring", 0, 0, tiled=True)
    ring_sum = jnp.sum(pieces, axis=0)
    reduced = ring_sum + lax.ppermute(ring_sum, "pair", [(0, 1), (1, 0)])
    spread = jnp.broadcast_to(reduced[None], (rings,) + reduced.shape)
    gathered = lax.all_to_all(spread, "ring", 0, 0, tiled=True).reshape(fields, row_count, 2 * KMAX)
    weighted = gathered * mode_weights(cut_rows, total_cols)[None]
    smooth = jnp.dot(weighted.reshape(-1, 2 * KMAX), basis.T, precision=lax.Precision.HIGHEST)
    return smooth.reshape(fields, row_count, col_count)


def ring_pairs(lat_count, lon_count, upward):
    half = lon_count // 2
    pairs = []
    for i in range(lat_count):
        for j in range(lon_count):
            north_going = (j < half) == upward
            if north_going:
                target = (i + 1, j) if i < lat_count - 1 else (i, (j + half) % lon_count)
            else:
                target = (i - 1, j) if i > 0 else (i, (j + half) % lon_count)
            pairs.append((i * lon_count + j, target[0] * lon_count + target[1]))
    return pairs


def ring_padded(block, flip_sign, band_index, lon_index, lat_count, lon_count):
    first = block[:, :, :2]
    last = block[:, :, -2:]
    far_half = lon_index >= lon_count // 2
    axes = ("lat",) + LON
    up = lax.ppermute(jnp.where(far_half, first, last), axes, ring_pairs(lat_count, lon_count, True))
    down = lax.ppermute(jnp.where(far_half, last, first), axes, ring_pairs(lat_count, lon_count, False))
    south = jnp.where(far_half, down, up)
    north = jnp.where(far_half, up, down)
    zero = jnp.zeros_like(south[:, :, :1])
    south_pole = jnp.concatenate([zero, flip_sign * south[:, :, :1]], axis=2)
    north_pole = jnp.concatenate([flip_sign * north[:, :, 1:], zero], axis=2)
    south = jnp.where(band_index == 0, south_pole, south)
    north = jnp.where(band_index == lat_count - 1, north_pole, north)
    return south, north


def lon_halos(block, lon_index, lon_count):
    first = block[..., :2]
    last = block[..., -2:]
    odd = lon_index % 2 == 1
    across = [(j, (j + 1) % lon_count if j % 2 else (j - 1) % lon_count) for j in range(lon_count)]
    far = lax.ppermute(jnp.where(odd, last, first), LON, across)
    near = lax.ppermute(jnp.where(odd, first, last), LON, [(j, j ^ 1) for j in range(lon_count)])
    west = jnp.where(odd, near, far)
    east = jnp.where(odd, far, near)
    return jnp.concatenate([west, block, east], axis=3)


def in_chip_order(core_index, own, other, axis):
    return jnp.where(
        core_index == 0,
        jnp.concatenate([own, other], axis=axis),
        jnp.concatenate([other, own], axis=axis),
    )


def local(base_state, section_state, cutoff, filter_mask):
    fields, levels, row_count, col_count = section_state.shape
    lat_count = lax.axis_size("lat")
    lon_count = lax.axis_size(LON)
    lon_index = lax.axis_index(LON)
    band_index = lax.axis_index("lat")
    core_index = lax.axis_index("core")
    swap = [(0, 1), (1, 0)]
    total_rows = row_count * lat_count
    total_cols = col_count * lon_count
    first_row = band_index * row_count
    flip_sign = jnp.where(jnp.arange(fields) < 2, -1.0, 1.0).astype(jnp.float32)[:, None, None, None]
    other_level = 1 - core_index
    own_level = lax.dynamic_index_in_dim(section_state, core_index, 1, keepdims=False)
    sibling_level = lax.ppermute(
        lax.dynamic_index_in_dim(section_state, other_level, 1, keepdims=False), "core", swap
    )
    south, north = ring_padded(section_state, flip_sign, band_index, lon_index, lat_count, lon_count)
    odd = core_index == 1
    across = [(j, (j + 1) % lon_count if j % 2 else (j - 1) % lon_count) for j in range(lon_count)]
    far = lax.ppermute(
        jnp.where(odd, section_state[..., -2:], section_state[..., :2]), LON, across
    )
    given = jnp.concatenate(
        [
            lax.dynamic_index_in_dim(south, other_level, 1, keepdims=False).reshape(fields, -1),
            lax.dynamic_index_in_dim(north, other_level, 1, keepdims=False).reshape(fields, -1),
            lax.dynamic_index_in_dim(far, other_level, 1, keepdims=False).reshape(fields, -1),
        ],
        axis=1,
    )
    got = lax.ppermute(given, "core", swap)
    edge = 2 * col_count
    got_south = got[:, :edge].reshape(fields, 2, col_count)
    got_north = got[:, edge : 2 * edge].reshape(fields, 2, col_count)
    got_far = got[:, 2 * edge :].reshape(fields, row_count, 2)
    own_far = lax.dynamic_index_in_dim(far, core_index, 1, keepdims=False)
    west = jnp.where(odd, got_far, own_far)
    east = jnp.where(odd, own_far, got_far)
    interior = in_chip_order(core_index, own_level, sibling_level, 2)
    chip_south = in_chip_order(
        core_index, lax.dynamic_index_in_dim(south, core_index, 1, keepdims=False), got_south, 2
    )
    chip_north = in_chip_order(
        core_index, lax.dynamic_index_in_dim(north, core_index, 1, keepdims=False), got_north, 2
    )
    lat_padded = jnp.concatenate([chip_south, interior, chip_north], axis=1)
    lon_padded = jnp.concatenate([west, interior, east], axis=2)
    face_cos = face_cosine(first_row, row_count, total_rows)
    cell_cos = cell_cosine(first_row, row_count, total_rows)
    lat_faces = interface(lat_padded, 1)
    lon_faces = interface(lon_padded, 2)
    north_flux = lat_faces[1][None] * lat_faces * face_cos[None, :, None]
    east_flux = lon_faces[0][None] * lon_faces
    tendency = (
        -(east_flux[..., 1:] - east_flux[..., :-1] + (north_flux[:, 1:] - north_flux[:, :-1]))
        / cell_cos[None, :, None]
    )
    own_mask = lax.dynamic_slice_in_dim(filter_mask, first_row, row_count)
    cut_rows = lax.dynamic_slice_in_dim(cutoff, first_row, row_count)
    chip_first_col = (lon_index - core_index) * col_count
    smooth = run_filter(tendency, cut_rows, chip_first_col, total_cols)
    filtered = jnp.where(own_mask[None, :, None] == 1, smooth, tendency)
    low_cols, high_cols = filtered[..., :col_count], filtered[..., col_count:]
    mine = jnp.where(odd, high_cols, low_cols)
    theirs = lax.ppermute(jnp.where(odd, low_cols, high_cols), "core", swap)
    level_zero = jnp.where(odd, theirs, mine)
    level_one = jnp.where(odd, mine, theirs)
    return base_state + section_weight * jnp.stack([level_zero, level_one], axis=1)


def solution(mesh):
    rings = mesh.shape["lon"] // 4
    mesh = jax.sharding.Mesh(mesh.devices.reshape(mesh.shape["lat"], rings, 2, 2), ("lat",) + LON)
    placed = (P(None, None, "lat", LON), P(None, None, "lat", LON), P(), P())
    return jax.shard_map(
        local, mesh=mesh, in_specs=placed, out_specs=P(None, None, "lat", LON), check_vma=False
    )
```

```python
import jax
import jax.numpy as jnp
from jax import lax
from jax.sharding import PartitionSpec as P

KMAX = 64
LON = ("ring", "pair", "core")


section_weight = 0.4


def passed_along(block, axis, distance):
    devices = range(lax.axis_size(axis))
    route = [((i - distance) % len(devices), i) for i in devices]
    return lax.ppermute(block, axis, route)


def padded_2(block, sides, width, periodic):
    for axis, dim in sides:
        count = lax.axis_size(axis)
        forward = [(i, i + 1) for i in range(count - 1)]
        if periodic:
            forward.append((count - 1, 0))
        backward = [(target, source) for source, target in forward]
        low = lax.ppermute(
            lax.slice_in_dim(block, block.shape[dim] - width, None, axis=dim), axis, forward
        )
        high = lax.ppermute(lax.slice_in_dim(block, 0, width, axis=dim), axis, backward)
        block = jnp.concatenate([low, block, high], axis=dim)
    return block


def interface(padded, along):
    length = padded.shape[along]
    outer_low = lax.slice_in_dim(padded, 0, length - 3, axis=along)
    inner_low = lax.slice_in_dim(padded, 1, length - 2, axis=along)
    inner_high = lax.slice_in_dim(padded, 2, length - 1, axis=along)
    outer_high = lax.slice_in_dim(padded, 3, length, axis=along)
    return (7.0 * (inner_low + inner_high) - (outer_low + outer_high)) / 12.0


def cell_cosine(first_row, row_count, total_rows):
    index_rows = first_row + jnp.arange(row_count, dtype=jnp.int32)
    return jnp.sin(jnp.pi * (index_rows.astype(jnp.float32) + 0.5) / total_rows)


def face_cosine(first_row, row_count, total_rows):
    index_faces = first_row + jnp.arange(row_count + 1, dtype=jnp.int32)
    raw_values = jnp.sin(jnp.pi * index_faces.astype(jnp.float32) / total_rows)
    return jnp.where((index_faces == 0) | (index_faces == total_rows), 0.0, raw_values)


def local_basis(first_col, col_count, total_cols):
    positions = first_col + jnp.arange(col_count, dtype=jnp.int32)
    product_index = positions[:, None] * jnp.arange(KMAX, dtype=jnp.int32)[None, :] % total_cols
    phases = product_index.astype(jnp.float32) * (2.0 * jnp.pi / total_cols)
    return jnp.concatenate([jnp.cos(phases), jnp.sin(phases)], axis=1)


def mode_weights(cut_rows, total_cols):
    mode_index = jnp.arange(2 * KMAX, dtype=jnp.int32) % KMAX
    mode_scale = jnp.where(mode_index == 0, 1.0 / total_cols, 2.0 / total_cols).astype(jnp.float32)
    return jnp.where(mode_index[None, :] < cut_rows[:, None], mode_scale[None, :], 0.0)


def swap_halves(block, core_index):
    half = block.shape[0] // 2
    low, high = block[:half], block[half:]
    keep = jnp.where(core_index == 0, low, high)
    give = jnp.where(core_index == 0, high, low)
    return keep, lax.ppermute(give, "core", [(0, 1), (1, 0)])


def doubling_gather(piece, rings):
    ring_index = lax.axis_index("ring")
    held = piece[None]
    bit = rings // 2
    while bit:
        theirs = lax.ppermute(held, "ring", [(r, r ^ bit) for r in range(rings)])
        upper = (ring_index & bit) != 0
        low = jnp.where(upper, theirs, held)
        high = jnp.where(upper, held, theirs)
        held = jnp.stack([low, high], axis=1).reshape((-1,) + piece.shape)
        bit //= 2
    return held


def run_filter(row_values, cut_rows, first_col, total_cols):
    fields, levels, row_count, col_count = row_values.shape
    rings = lax.axis_size("ring")
    core_index = lax.axis_index("core")
    basis = local_basis(first_col, col_count, total_cols)
    flat = row_values.reshape(fields * levels * row_count, col_count)
    partial = jnp.dot(flat, basis, precision=lax.Precision.HIGHEST)
    keep, got = swap_halves(partial, core_index)
    chip_sum = (keep + got).reshape(rings, -1, 2 * KMAX)
    pieces = lax.all_to_all(chip_sum, "ring", 0, 0, tiled=True)
    ring_sum = jnp.sum(pieces, axis=0)
    reduced = ring_sum + lax.ppermute(ring_sum, "pair", [(0, 1), (1, 0)])
    gathered = doubling_gather(reduced, rings).reshape(-1, 2 * KMAX)
    other = lax.ppermute(gathered, "core", [(0, 1), (1, 0)])
    low = jnp.where(core_index == 0, gathered, other)
    high = jnp.where(core_index == 0, other, gathered)
    coefficients = jnp.concatenate([low, high], axis=0).reshape(fields * levels, row_count, 2 * KMAX)
    weighted = coefficients * mode_weights(cut_rows, total_cols)[None]
    smooth = jnp.dot(weighted.reshape(-1, 2 * KMAX), basis.T, precision=lax.Precision.HIGHEST)
    return smooth.reshape(fields, levels, row_count, col_count)


def ring_pairs(lat_count, lon_count, upward):
    half = lon_count // 2
    pairs = []
    for i in range(lat_count):
        for j in range(lon_count):
            north_going = (j < half) == upward
            if north_going:
                target = (i + 1, j) if i < lat_count - 1 else (i, (j + half) % lon_count)
            else:
                target = (i - 1, j) if i > 0 else (i, (j + half) % lon_count)
            pairs.append((i * lon_count + j, target[0] * lon_count + target[1]))
    return pairs


def ring_padded(block, flip_sign, band_index, lon_index, lat_count, lon_count):
    first = block[:, :, :2]
    last = block[:, :, -2:]
    far_half = lon_index >= lon_count // 2
    axes = ("lat",) + LON
    up = lax.ppermute(jnp.where(far_half, first, last), axes, ring_pairs(lat_count, lon_count, True))
    down = lax.ppermute(jnp.where(far_half, last, first), axes, ring_pairs(lat_count, lon_count, False))
    south = jnp.where(far_half, down, up)
    north = jnp.where(far_half, up, down)
    zero = jnp.zeros_like(south[:, :, :1])
    south_pole = jnp.concatenate([zero, flip_sign * south[:, :, :1]], axis=2)
    north_pole = jnp.concatenate([flip_sign * north[:, :, 1:], zero], axis=2)
    south = jnp.where(band_index == 0, south_pole, south)
    north = jnp.where(band_index == lat_count - 1, north_pole, north)
    return jnp.concatenate([south, block, north], axis=2)


def lon_halos(block, lon_index, lon_count):
    first = block[..., :2]
    last = block[..., -2:]
    odd = lon_index % 2 == 1
    across = [(j, (j + 1) % lon_count if j % 2 else (j - 1) % lon_count) for j in range(lon_count)]
    far = lax.ppermute(jnp.where(odd, last, first), LON, across)
    near = lax.ppermute(jnp.where(odd, first, last), LON, [(j, j ^ 1) for j in range(lon_count)])
    west = jnp.where(odd, near, far)
    east = jnp.where(odd, far, near)
    return jnp.concatenate([west, block, east], axis=3)


def local(base_state, section_state, cutoff, filter_mask):
    fields, levels, row_count, col_count = section_state.shape
    lat_count = lax.axis_size("lat")
    lon_count = lax.axis_size(LON)
    lon_index = lax.axis_index(LON)
    band_index = lax.axis_index("lat")
    total_rows = row_count * lat_count
    total_cols = col_count * lon_count
    first_row = band_index * row_count
    flip_sign = jnp.where(jnp.arange(fields) < 2, -1.0, 1.0).astype(jnp.float32)[:, None, None, None]
    lat_padded = ring_padded(section_state, flip_sign, band_index, lon_index, lat_count, lon_count)
    lon_padded = lon_halos(section_state, lon_index, lon_count)
    face_cos = face_cosine(first_row, row_count, total_rows)
    cell_cos = cell_cosine(first_row, row_count, total_rows)
    lat_faces = interface(lat_padded, 2)
    lon_faces = interface(lon_padded, 3)
    north_flux = lat_faces[1][None] * lat_faces * face_cos[None, None, :, None]
    east_flux = lon_faces[0][None] * lon_faces
    tendency = (
        -(east_flux[..., 1:] - east_flux[..., :-1] + (north_flux[:, :, 1:] - north_flux[:, :, :-1]))
        / cell_cos[None, None, :, None]
    )
    own_mask = lax.dynamic_slice_in_dim(filter_mask, first_row, row_count)
    cut_rows = lax.dynamic_slice_in_dim(cutoff, first_row, row_count)
    smooth = run_filter(tendency, cut_rows, lon_index * col_count, total_cols)
    filtered = jnp.where(own_mask[None, None, :, None] == 1, smooth, tendency)
    return base_state + section_weight * filtered


def solution(mesh):
    rings = mesh.shape["lon"] // 4
    mesh = jax.sharding.Mesh(mesh.devices.reshape(mesh.shape["lat"], rings, 2, 2), ("lat",) + LON)
    placed = (P(None, None, "lat", LON), P(None, None, "lat", LON), P(), P())
    return jax.shard_map(
        local, mesh=mesh, in_specs=placed, out_specs=P(None, None, "lat", LON), check_vma=False
    )
```

```python
import jax
import jax.numpy as jnp
from jax import lax
from jax.sharding import PartitionSpec as P

KMAX = 64
LON = ("ring", "pair", "core")


section_weight = 0.4


def passed_along(block, axis, distance):
    devices = range(lax.axis_size(axis))
    route = [((i - distance) % len(devices), i) for i in devices]
    return lax.ppermute(block, axis, route)


def padded_2(block, sides, width, periodic):
    for axis, dim in sides:
        count = lax.axis_size(axis)
        forward = [(i, i + 1) for i in range(count - 1)]
        if periodic:
            forward.append((count - 1, 0))
        backward = [(target, source) for source, target in forward]
        low = lax.ppermute(
            lax.slice_in_dim(block, block.shape[dim] - width, None, axis=dim), axis, forward
        )
        high = lax.ppermute(lax.slice_in_dim(block, 0, width, axis=dim), axis, backward)
        block = jnp.concatenate([low, block, high], axis=dim)
    return block


def interface(padded, along):
    length = padded.shape[along]
    outer_low = lax.slice_in_dim(padded, 0, length - 3, axis=along)
    inner_low = lax.slice_in_dim(padded, 1, length - 2, axis=along)
    inner_high = lax.slice_in_dim(padded, 2, length - 1, axis=along)
    outer_high = lax.slice_in_dim(padded, 3, length, axis=along)
    return (7.0 * (inner_low + inner_high) - (outer_low + outer_high)) / 12.0


def cell_cosine(first_row, row_count, total_rows):
    index_rows = first_row + jnp.arange(row_count, dtype=jnp.int32)
    return jnp.sin(jnp.pi * (index_rows.astype(jnp.float32) + 0.5) / total_rows)


def face_cosine(first_row, row_count, total_rows):
    index_faces = first_row + jnp.arange(row_count + 1, dtype=jnp.int32)
    raw_values = jnp.sin(jnp.pi * index_faces.astype(jnp.float32) / total_rows)
    return jnp.where((index_faces == 0) | (index_faces == total_rows), 0.0, raw_values)


def local_basis(first_col, col_count, total_cols):
    positions = first_col + jnp.arange(col_count, dtype=jnp.int32)
    product_index = positions[:, None] * jnp.arange(KMAX, dtype=jnp.int32)[None, :] % total_cols
    phases = product_index.astype(jnp.float32) * (2.0 * jnp.pi / total_cols)
    return jnp.concatenate([jnp.cos(phases), jnp.sin(phases)], axis=1)


def mode_weights(cut_rows, total_cols):
    mode_index = jnp.arange(2 * KMAX, dtype=jnp.int32) % KMAX
    mode_scale = jnp.where(mode_index == 0, 1.0 / total_cols, 2.0 / total_cols).astype(jnp.float32)
    return jnp.where(mode_index[None, :] < cut_rows[:, None], mode_scale[None, :], 0.0)


def swap_halves(block, core_index):
    half = block.shape[0] // 2
    low, high = block[:half], block[half:]
    keep = jnp.where(core_index == 0, low, high)
    give = jnp.where(core_index == 0, high, low)
    return keep, lax.ppermute(give, "core", [(0, 1), (1, 0)])


def run_filter(row_values, cut_rows, first_col, total_cols):
    fields, levels, row_count, col_count = row_values.shape
    rings = lax.axis_size("ring")
    core_index = lax.axis_index("core")
    basis = local_basis(first_col, col_count, total_cols)
    flat = row_values.reshape(fields * levels * row_count, col_count)
    partial = jnp.dot(flat, basis, precision=lax.Precision.HIGHEST)
    keep, got = swap_halves(partial, core_index)
    chips = rings * lax.axis_size("pair")
    chip_sum = (keep + got).reshape(chips, -1, 2 * KMAX)
    pieces = lax.all_to_all(chip_sum, ("ring", "pair"), 0, 0, tiled=True)
    reduced = jnp.sum(pieces, axis=0)
    spread = jnp.broadcast_to(reduced[None], (chips,) + reduced.shape)
    gathered = lax.all_to_all(spread, ("ring", "pair"), 0, 0, tiled=True).reshape(-1, 2 * KMAX)
    other = lax.ppermute(gathered, "core", [(0, 1), (1, 0)])
    low = jnp.where(core_index == 0, gathered, other)
    high = jnp.where(core_index == 0, other, gathered)
    coefficients = jnp.concatenate([low, high], axis=0).reshape(fields * levels, row_count, 2 * KMAX)
    weighted = coefficients * mode_weights(cut_rows, total_cols)[None]
    smooth = jnp.dot(weighted.reshape(-1, 2 * KMAX), basis.T, precision=lax.Precision.HIGHEST)
    return smooth.reshape(fields, levels, row_count, col_count)


def ring_pairs(lat_count, lon_count, upward):
    half = lon_count // 2
    pairs = []
    for i in range(lat_count):
        for j in range(lon_count):
            north_going = (j < half) == upward
            if north_going:
                target = (i + 1, j) if i < lat_count - 1 else (i, (j + half) % lon_count)
            else:
                target = (i - 1, j) if i > 0 else (i, (j + half) % lon_count)
            pairs.append((i * lon_count + j, target[0] * lon_count + target[1]))
    return pairs


def ring_padded(block, flip_sign, band_index, lon_index, lat_count, lon_count):
    first = block[:, :, :2]
    last = block[:, :, -2:]
    far_half = lon_index >= lon_count // 2
    axes = ("lat",) + LON
    up = lax.ppermute(jnp.where(far_half, first, last), axes, ring_pairs(lat_count, lon_count, True))
    down = lax.ppermute(jnp.where(far_half, last, first), axes, ring_pairs(lat_count, lon_count, False))
    south = jnp.where(far_half, down, up)
    north = jnp.where(far_half, up, down)
    zero = jnp.zeros_like(south[:, :, :1])
    south_pole = jnp.concatenate([zero, flip_sign * south[:, :, :1]], axis=2)
    north_pole = jnp.concatenate([flip_sign * north[:, :, 1:], zero], axis=2)
    south = jnp.where(band_index == 0, south_pole, south)
    north = jnp.where(band_index == lat_count - 1, north_pole, north)
    return jnp.concatenate([south, block, north], axis=2)


def lon_halos(block, lon_index, lon_count):
    first = block[..., :2]
    last = block[..., -2:]
    odd = lon_index % 2 == 1
    across = [(j, (j + 1) % lon_count if j % 2 else (j - 1) % lon_count) for j in range(lon_count)]
    far = lax.ppermute(jnp.where(odd, last, first), LON, across)
    near = lax.ppermute(jnp.where(odd, first, last), LON, [(j, j ^ 1) for j in range(lon_count)])
    west = jnp.where(odd, near, far)
    east = jnp.where(odd, far, near)
    return jnp.concatenate([west, block, east], axis=3)


def local(base_state, section_state, cutoff, filter_mask):
    fields, levels, row_count, col_count = section_state.shape
    lat_count = lax.axis_size("lat")
    lon_count = lax.axis_size(LON)
    lon_index = lax.axis_index(LON)
    band_index = lax.axis_index("lat")
    total_rows = row_count * lat_count
    total_cols = col_count * lon_count
    first_row = band_index * row_count
    flip_sign = jnp.where(jnp.arange(fields) < 2, -1.0, 1.0).astype(jnp.float32)[:, None, None, None]
    lat_padded = ring_padded(section_state, flip_sign, band_index, lon_index, lat_count, lon_count)
    lon_padded = lon_halos(section_state, lon_index, lon_count)
    face_cos = face_cosine(first_row, row_count, total_rows)
    cell_cos = cell_cosine(first_row, row_count, total_rows)
    lat_faces = interface(lat_padded, 2)
    lon_faces = interface(lon_padded, 3)
    north_flux = lat_faces[1][None] * lat_faces * face_cos[None, None, :, None]
    east_flux = lon_faces[0][None] * lon_faces
    tendency = (
        -(east_flux[..., 1:] - east_flux[..., :-1] + (north_flux[:, :, 1:] - north_flux[:, :, :-1]))
        / cell_cos[None, None, :, None]
    )
    own_mask = lax.dynamic_slice_in_dim(filter_mask, first_row, row_count)
    cut_rows = lax.dynamic_slice_in_dim(cutoff, first_row, row_count)
    smooth = run_filter(tendency, cut_rows, lon_index * col_count, total_cols)
    filtered = jnp.where(own_mask[None, None, :, None] == 1, smooth, tendency)
    return base_state + section_weight * filtered


def solution(mesh):
    rings = mesh.shape["lon"] // 4
    mesh = jax.sharding.Mesh(mesh.devices.reshape(mesh.shape["lat"], rings, 2, 2), ("lat",) + LON)
    placed = (P(None, None, "lat", LON), P(None, None, "lat", LON), P(), P())
    return jax.shard_map(
        local, mesh=mesh, in_specs=placed, out_specs=P(None, None, "lat", LON), check_vma=False
    )
```

```python
import jax
import jax.numpy as jnp
from jax import lax
from jax.sharding import PartitionSpec as P

KMAX = 64
LON = ("ring", "pair", "core")


section_weight = 0.4


def passed_along(block, axis, distance):
    devices = range(lax.axis_size(axis))
    route = [((i - distance) % len(devices), i) for i in devices]
    return lax.ppermute(block, axis, route)


def padded_2(block, sides, width, periodic):
    for axis, dim in sides:
        count = lax.axis_size(axis)
        forward = [(i, i + 1) for i in range(count - 1)]
        if periodic:
            forward.append((count - 1, 0))
        backward = [(target, source) for source, target in forward]
        low = lax.ppermute(
            lax.slice_in_dim(block, block.shape[dim] - width, None, axis=dim), axis, forward
        )
        high = lax.ppermute(lax.slice_in_dim(block, 0, width, axis=dim), axis, backward)
        block = jnp.concatenate([low, block, high], axis=dim)
    return block


def interface(padded, along):
    length = padded.shape[along]
    outer_low = lax.slice_in_dim(padded, 0, length - 3, axis=along)
    inner_low = lax.slice_in_dim(padded, 1, length - 2, axis=along)
    inner_high = lax.slice_in_dim(padded, 2, length - 1, axis=along)
    outer_high = lax.slice_in_dim(padded, 3, length, axis=along)
    return (7.0 * (inner_low + inner_high) - (outer_low + outer_high)) / 12.0


def cell_cosine(first_row, row_count, total_rows):
    index_rows = first_row + jnp.arange(row_count, dtype=jnp.int32)
    return jnp.sin(jnp.pi * (index_rows.astype(jnp.float32) + 0.5) / total_rows)


def face_cosine(first_row, row_count, total_rows):
    index_faces = first_row + jnp.arange(row_count + 1, dtype=jnp.int32)
    raw_values = jnp.sin(jnp.pi * index_faces.astype(jnp.float32) / total_rows)
    return jnp.where((index_faces == 0) | (index_faces == total_rows), 0.0, raw_values)


def local_basis(first_col, col_count, total_cols):
    positions = first_col + jnp.arange(col_count, dtype=jnp.int32)
    product_index = positions[:, None] * jnp.arange(KMAX, dtype=jnp.int32)[None, :] % total_cols
    phases = product_index.astype(jnp.float32) * (2.0 * jnp.pi / total_cols)
    return jnp.concatenate([jnp.cos(phases), jnp.sin(phases)], axis=1)


def mode_weights(cut_rows, total_cols):
    mode_index = jnp.arange(2 * KMAX, dtype=jnp.int32) % KMAX
    mode_scale = jnp.where(mode_index == 0, 1.0 / total_cols, 2.0 / total_cols).astype(jnp.float32)
    return jnp.where(mode_index[None, :] < cut_rows[:, None], mode_scale[None, :], 0.0)


def swap_halves(block, core_index):
    half = block.shape[0] // 2
    low, high = block[:half], block[half:]
    keep = jnp.where(core_index == 0, low, high)
    give = jnp.where(core_index == 0, high, low)
    return keep, lax.ppermute(give, "core", [(0, 1), (1, 0)])


def run_filter(row_values, cut_rows, first_col, total_cols):
    fields, levels, row_count, col_count = row_values.shape
    rings = lax.axis_size("ring")
    core_index = lax.axis_index("core")
    basis = local_basis(first_col, col_count, total_cols)
    flat = row_values.reshape(fields * levels * row_count, col_count)
    partial = jnp.dot(flat, basis, precision=lax.Precision.HIGH)
    keep, got = swap_halves(partial, core_index)
    chip_sum = (keep + got).reshape(rings, -1, 2 * KMAX)
    pieces = lax.all_to_all(chip_sum, "ring", 0, 0, tiled=True)
    ring_sum = jnp.sum(pieces, axis=0)
    reduced = ring_sum + lax.ppermute(ring_sum, "pair", [(0, 1), (1, 0)])
    spread = jnp.broadcast_to(reduced[None], (rings,) + reduced.shape)
    gathered = lax.all_to_all(spread, "ring", 0, 0, tiled=True).reshape(-1, 2 * KMAX)
    other = lax.ppermute(gathered, "core", [(0, 1), (1, 0)])
    low = jnp.where(core_index == 0, gathered, other)
    high = jnp.where(core_index == 0, other, gathered)
    coefficients = jnp.concatenate([low, high], axis=0).reshape(fields * levels, row_count, 2 * KMAX)
    weighted = coefficients * mode_weights(cut_rows, total_cols)[None]
    smooth = jnp.dot(weighted.reshape(-1, 2 * KMAX), basis.T, precision=lax.Precision.HIGH)
    return smooth.reshape(fields, levels, row_count, col_count)


def ring_pairs(lat_count, lon_count, upward):
    half = lon_count // 2
    pairs = []
    for i in range(lat_count):
        for j in range(lon_count):
            north_going = (j < half) == upward
            if north_going:
                target = (i + 1, j) if i < lat_count - 1 else (i, (j + half) % lon_count)
            else:
                target = (i - 1, j) if i > 0 else (i, (j + half) % lon_count)
            pairs.append((i * lon_count + j, target[0] * lon_count + target[1]))
    return pairs


def ring_padded(block, flip_sign, band_index, lon_index, lat_count, lon_count):
    first = block[:, :, :2]
    last = block[:, :, -2:]
    far_half = lon_index >= lon_count // 2
    axes = ("lat",) + LON
    up = lax.ppermute(jnp.where(far_half, first, last), axes, ring_pairs(lat_count, lon_count, True))
    down = lax.ppermute(jnp.where(far_half, last, first), axes, ring_pairs(lat_count, lon_count, False))
    south = jnp.where(far_half, down, up)
    north = jnp.where(far_half, up, down)
    zero = jnp.zeros_like(south[:, :, :1])
    south_pole = jnp.concatenate([zero, flip_sign * south[:, :, :1]], axis=2)
    north_pole = jnp.concatenate([flip_sign * north[:, :, 1:], zero], axis=2)
    south = jnp.where(band_index == 0, south_pole, south)
    north = jnp.where(band_index == lat_count - 1, north_pole, north)
    return jnp.concatenate([south, block, north], axis=2)


def lon_halos(block, lon_index, lon_count):
    first = block[..., :2]
    last = block[..., -2:]
    odd = lon_index % 2 == 1
    across = [(j, (j + 1) % lon_count if j % 2 else (j - 1) % lon_count) for j in range(lon_count)]
    far = lax.ppermute(jnp.where(odd, last, first), LON, across)
    near = lax.ppermute(jnp.where(odd, first, last), LON, [(j, j ^ 1) for j in range(lon_count)])
    west = jnp.where(odd, near, far)
    east = jnp.where(odd, far, near)
    return jnp.concatenate([west, block, east], axis=3)


def local(base_state, section_state, cutoff, filter_mask):
    fields, levels, row_count, col_count = section_state.shape
    lat_count = lax.axis_size("lat")
    lon_count = lax.axis_size(LON)
    lon_index = lax.axis_index(LON)
    band_index = lax.axis_index("lat")
    total_rows = row_count * lat_count
    total_cols = col_count * lon_count
    first_row = band_index * row_count
    flip_sign = jnp.where(jnp.arange(fields) < 2, -1.0, 1.0).astype(jnp.float32)[:, None, None, None]
    lat_padded = ring_padded(section_state, flip_sign, band_index, lon_index, lat_count, lon_count)
    lon_padded = lon_halos(section_state, lon_index, lon_count)
    face_cos = face_cosine(first_row, row_count, total_rows)
    cell_cos = cell_cosine(first_row, row_count, total_rows)
    lat_faces = interface(lat_padded, 2)
    lon_faces = interface(lon_padded, 3)
    north_flux = lat_faces[1][None] * lat_faces * face_cos[None, None, :, None]
    east_flux = lon_faces[0][None] * lon_faces
    tendency = (
        -(east_flux[..., 1:] - east_flux[..., :-1] + (north_flux[:, :, 1:] - north_flux[:, :, :-1]))
        / cell_cos[None, None, :, None]
    )
    own_mask = lax.dynamic_slice_in_dim(filter_mask, first_row, row_count)
    cut_rows = lax.dynamic_slice_in_dim(cutoff, first_row, row_count)
    smooth = run_filter(tendency, cut_rows, lon_index * col_count, total_cols)
    filtered = jnp.where(own_mask[None, None, :, None] == 1, smooth, tendency)
    return base_state + section_weight * filtered


def solution(mesh):
    rings = mesh.shape["lon"] // 4
    mesh = jax.sharding.Mesh(mesh.devices.reshape(mesh.shape["lat"], rings, 2, 2), ("lat",) + LON)
    placed = (P(None, None, "lat", LON), P(None, None, "lat", LON), P(), P())
    return jax.shard_map(
        local, mesh=mesh, in_specs=placed, out_specs=P(None, None, "lat", LON), check_vma=False
    )
```

```python
import jax
import jax.numpy as jnp
from jax import lax
from jax.sharding import PartitionSpec as P

KMAX = 64
LON = ("ring", "pair", "core")


section_weight = 0.4


def passed_along(block, axis, distance):
    devices = range(lax.axis_size(axis))
    route = [((i - distance) % len(devices), i) for i in devices]
    return lax.ppermute(block, axis, route)


def padded_2(block, sides, width, periodic):
    for axis, dim in sides:
        count = lax.axis_size(axis)
        forward = [(i, i + 1) for i in range(count - 1)]
        if periodic:
            forward.append((count - 1, 0))
        backward = [(target, source) for source, target in forward]
        low = lax.ppermute(
            lax.slice_in_dim(block, block.shape[dim] - width, None, axis=dim), axis, forward
        )
        high = lax.ppermute(lax.slice_in_dim(block, 0, width, axis=dim), axis, backward)
        block = jnp.concatenate([low, block, high], axis=dim)
    return block


def interface(padded, along):
    length = padded.shape[along]
    outer_low = lax.slice_in_dim(padded, 0, length - 3, axis=along)
    inner_low = lax.slice_in_dim(padded, 1, length - 2, axis=along)
    inner_high = lax.slice_in_dim(padded, 2, length - 1, axis=along)
    outer_high = lax.slice_in_dim(padded, 3, length, axis=along)
    return (7.0 * (inner_low + inner_high) - (outer_low + outer_high)) / 12.0


def cell_cosine(first_row, row_count, total_rows):
    index_rows = first_row + jnp.arange(row_count, dtype=jnp.int32)
    return jnp.sin(jnp.pi * (index_rows.astype(jnp.float32) + 0.5) / total_rows)


def face_cosine(first_row, row_count, total_rows):
    index_faces = first_row + jnp.arange(row_count + 1, dtype=jnp.int32)
    raw_values = jnp.sin(jnp.pi * index_faces.astype(jnp.float32) / total_rows)
    return jnp.where((index_faces == 0) | (index_faces == total_rows), 0.0, raw_values)


def local_basis(first_col, col_count, total_cols):
    positions = first_col + jnp.arange(col_count, dtype=jnp.int32)
    product_index = positions[:, None] * jnp.arange(KMAX, dtype=jnp.int32)[None, :] % total_cols
    phases = product_index.astype(jnp.float32) * (2.0 * jnp.pi / total_cols)
    return jnp.concatenate([jnp.cos(phases), jnp.sin(phases)], axis=1)


def mode_weights(cut_rows, total_cols):
    mode_index = jnp.arange(2 * KMAX, dtype=jnp.int32) % KMAX
    mode_scale = jnp.where(mode_index == 0, 1.0 / total_cols, 2.0 / total_cols).astype(jnp.float32)
    return jnp.where(mode_index[None, :] < cut_rows[:, None], mode_scale[None, :], 0.0)


def swap_halves(block, core_index):
    half = block.shape[0] // 2
    low, high = block[:half], block[half:]
    keep = jnp.where(core_index == 0, low, high)
    give = jnp.where(core_index == 0, high, low)
    return keep, lax.ppermute(give, "core", [(0, 1), (1, 0)])


def run_filter(row_values, cut_rows, first_col, total_cols):
    fields, levels, row_count, col_count = row_values.shape
    rings = lax.axis_size("ring")
    core_index = lax.axis_index("core")
    basis = local_basis(first_col, col_count, total_cols)
    flat = row_values.reshape(fields * levels * row_count, col_count)
    partial = jnp.dot(flat, basis, precision=lax.Precision.HIGH)
    keep, got = swap_halves(partial, core_index)
    chip_sum = (keep + got).reshape(rings, -1, 2 * KMAX)
    pieces = lax.all_to_all(chip_sum, "ring", 0, 0, tiled=True)
    ring_sum = jnp.sum(pieces, axis=0)
    reduced = ring_sum + lax.ppermute(ring_sum, "pair", [(0, 1), (1, 0)])
    spread = jnp.broadcast_to(reduced[None], (rings,) + reduced.shape)
    gathered = lax.all_to_all(spread, "ring", 0, 0, tiled=True).reshape(-1, 2 * KMAX)
    other = lax.ppermute(gathered, "core", [(0, 1), (1, 0)])
    low = jnp.where(core_index == 0, gathered, other)
    high = jnp.where(core_index == 0, other, gathered)
    coefficients = jnp.concatenate([low, high], axis=0).reshape(fields * levels, row_count, 2 * KMAX)
    weighted = coefficients * mode_weights(cut_rows, total_cols)[None]
    smooth = jnp.dot(weighted.reshape(-1, 2 * KMAX), basis.T, precision=lax.Precision.HIGH)
    return smooth.reshape(fields, levels, row_count, col_count)


def ring_pairs(lat_count, lon_count, upward):
    half = lon_count // 2
    pairs = []
    for i in range(lat_count):
        for j in range(lon_count):
            north_going = (j < half) == upward
            if north_going:
                target = (i + 1, j) if i < lat_count - 1 else (i, (j + half) % lon_count)
            else:
                target = (i - 1, j) if i > 0 else (i, (j + half) % lon_count)
            pairs.append((i * lon_count + j, target[0] * lon_count + target[1]))
    return pairs


def ring_padded(block, flip_sign, band_index, lon_index, lat_count, lon_count):
    first = block[:, :, :2]
    last = block[:, :, -2:]
    far_half = lon_index >= lon_count // 2
    axes = ("lat",) + LON
    up = lax.ppermute(jnp.where(far_half, first, last), axes, ring_pairs(lat_count, lon_count, True))
    down = lax.ppermute(jnp.where(far_half, last, first), axes, ring_pairs(lat_count, lon_count, False))
    south = jnp.where(far_half, down, up)
    north = jnp.where(far_half, up, down)
    zero = jnp.zeros_like(south[:, :, :1])
    south_pole = jnp.concatenate([zero, flip_sign * south[:, :, :1]], axis=2)
    north_pole = jnp.concatenate([flip_sign * north[:, :, 1:], zero], axis=2)
    south = jnp.where(band_index == 0, south_pole, south)
    north = jnp.where(band_index == lat_count - 1, north_pole, north)
    return jnp.concatenate([south, block, north], axis=2)


def lon_halos(block, lon_index, lon_count):
    first = block[..., :2]
    last = block[..., -2:]
    odd = lon_index % 2 == 1
    across = [(j, (j + 1) % lon_count if j % 2 else (j - 1) % lon_count) for j in range(lon_count)]
    far = lax.ppermute(jnp.where(odd, last, first), LON, across)
    near = lax.ppermute(jnp.where(odd, first, last), LON, [(j, j ^ 1) for j in range(lon_count)])
    west = jnp.where(odd, near, far)
    east = jnp.where(odd, far, near)
    return jnp.concatenate([west, block, east], axis=3)


def local(base_state, section_state, cutoff, filter_mask):
    fields, levels, row_count, col_count = section_state.shape
    lat_count = lax.axis_size("lat")
    lon_count = lax.axis_size(LON)
    lon_index = lax.axis_index(LON)
    band_index = lax.axis_index("lat")
    total_rows = row_count * lat_count
    total_cols = col_count * lon_count
    first_row = band_index * row_count
    flip_sign = jnp.where(jnp.arange(fields) < 2, -1.0, 1.0).astype(jnp.float32)[:, None, None, None]
    lat_padded = ring_padded(section_state, flip_sign, band_index, lon_index, lat_count, lon_count)
    lon_padded = lon_halos(section_state, lon_index, lon_count)
    face_cos = face_cosine(first_row, row_count, total_rows)
    cell_cos = cell_cosine(first_row, row_count, total_rows)
    lat_faces = interface(lat_padded, 2)
    lon_faces = interface(lon_padded, 3)
    north_flux = lat_faces[1][None] * lat_faces * face_cos[None, None, :, None]
    east_flux = lon_faces[0][None] * lon_faces
    tendency = (
        -(east_flux[..., 1:] - east_flux[..., :-1] + (north_flux[:, :, 1:] - north_flux[:, :, :-1]))
        / cell_cos[None, None, :, None]
    )
    packed = lax.dynamic_slice_in_dim(cutoff * 2 + filter_mask, first_row, row_count)
    own_mask = packed % 2
    cut_rows = packed // 2
    smooth = run_filter(tendency, cut_rows, lon_index * col_count, total_cols)
    filtered = jnp.where(own_mask[None, None, :, None] == 1, smooth, tendency)
    return base_state + section_weight * filtered


def solution(mesh):
    rings = mesh.shape["lon"] // 4
    mesh = jax.sharding.Mesh(mesh.devices.reshape(mesh.shape["lat"], rings, 2, 2), ("lat",) + LON)
    placed = (P(None, None, "lat", LON), P(None, None, "lat", LON), P(), P())
    return jax.shard_map(
        local, mesh=mesh, in_specs=placed, out_specs=P(None, None, "lat", LON), check_vma=False
    )
```

```python
import jax
import jax.numpy as jnp
from jax import lax
from jax.sharding import PartitionSpec as P

KMAX = 64
LON = ("ring", "pair", "core")


section_weight = 0.4


def passed_along(block, axis, distance):
    devices = range(lax.axis_size(axis))
    route = [((i - distance) % len(devices), i) for i in devices]
    return lax.ppermute(block, axis, route)


def padded_2(block, sides, width, periodic):
    for axis, dim in sides:
        count = lax.axis_size(axis)
        forward = [(i, i + 1) for i in range(count - 1)]
        if periodic:
            forward.append((count - 1, 0))
        backward = [(target, source) for source, target in forward]
        low = lax.ppermute(
            lax.slice_in_dim(block, block.shape[dim] - width, None, axis=dim), axis, forward
        )
        high = lax.ppermute(lax.slice_in_dim(block, 0, width, axis=dim), axis, backward)
        block = jnp.concatenate([low, block, high], axis=dim)
    return block


def interface(padded, along):
    length = padded.shape[along]
    outer_low = lax.slice_in_dim(padded, 0, length - 3, axis=along)
    inner_low = lax.slice_in_dim(padded, 1, length - 2, axis=along)
    inner_high = lax.slice_in_dim(padded, 2, length - 1, axis=along)
    outer_high = lax.slice_in_dim(padded, 3, length, axis=along)
    return (7.0 * (inner_low + inner_high) - (outer_low + outer_high)) / 12.0


def cell_cosine(first_row, row_count, total_rows):
    index_rows = first_row + jnp.arange(row_count, dtype=jnp.int32)
    return jnp.sin(jnp.pi * (index_rows.astype(jnp.float32) + 0.5) / total_rows)


def face_cosine(first_row, row_count, total_rows):
    index_faces = first_row + jnp.arange(row_count + 1, dtype=jnp.int32)
    raw_values = jnp.sin(jnp.pi * index_faces.astype(jnp.float32) / total_rows)
    return jnp.where((index_faces == 0) | (index_faces == total_rows), 0.0, raw_values)


def local_basis(first_col, col_count, total_cols):
    positions = first_col + jnp.arange(col_count, dtype=jnp.int32)
    product_index = positions[:, None] * jnp.arange(KMAX, dtype=jnp.int32)[None, :] % total_cols
    phases = product_index.astype(jnp.float32) * (2.0 * jnp.pi / total_cols)
    return jnp.concatenate([jnp.cos(phases), jnp.sin(phases)], axis=1)


def mode_weights(cut_rows, total_cols):
    mode_index = jnp.arange(2 * KMAX, dtype=jnp.int32) % KMAX
    mode_scale = jnp.where(mode_index == 0, 1.0 / total_cols, 2.0 / total_cols).astype(jnp.float32)
    return jnp.where(mode_index[None, :] < cut_rows[:, None], mode_scale[None, :], 0.0)


def swap_halves(block, core_index):
    half = block.shape[0] // 2
    low, high = block[:half], block[half:]
    keep = jnp.where(core_index == 0, low, high)
    give = jnp.where(core_index == 0, high, low)
    return keep, lax.ppermute(give, "core", [(0, 1), (1, 0)])


def run_filter(row_values, cut_rows, first_col, total_cols):
    fields, levels, row_count, col_count = row_values.shape
    rings = lax.axis_size("ring")
    core_index = lax.axis_index("core")
    basis = local_basis(first_col, col_count, total_cols)
    flat = row_values.reshape(fields * levels * row_count, col_count)
    partial = jnp.dot(flat, basis, precision=lax.Precision.HIGH)
    keep, got = swap_halves(partial, core_index)
    chip_sum = (keep + got).reshape(rings, -1, 2 * KMAX)
    pieces = lax.all_to_all(chip_sum, "ring", 0, 0, tiled=True)
    ring_sum = jnp.sum(pieces, axis=0)
    reduced = ring_sum + lax.ppermute(ring_sum, "pair", [(0, 1), (1, 0)])
    spread = jnp.broadcast_to(reduced[None], (rings,) + reduced.shape)
    gathered = lax.all_to_all(spread, "ring", 0, 0, tiled=True).reshape(-1, 2 * KMAX)
    other = lax.ppermute(gathered, "core", [(0, 1), (1, 0)])
    weights = mode_weights(cut_rows, total_cols)

    def synthesize(half):
        weighted = half.reshape(-1, row_count, 2 * KMAX) * weights[None]
        return jnp.dot(weighted.reshape(-1, 2 * KMAX), basis.T, precision=lax.Precision.HIGH)

    own, theirs = synthesize(gathered), synthesize(other)
    smooth = jnp.where(
        core_index == 0,
        jnp.concatenate([own, theirs], axis=0),
        jnp.concatenate([theirs, own], axis=0),
    )
    return smooth.reshape(fields, levels, row_count, col_count)


def ring_pairs(lat_count, lon_count, upward):
    half = lon_count // 2
    pairs = []
    for i in range(lat_count):
        for j in range(lon_count):
            north_going = (j < half) == upward
            if north_going:
                target = (i + 1, j) if i < lat_count - 1 else (i, (j + half) % lon_count)
            else:
                target = (i - 1, j) if i > 0 else (i, (j + half) % lon_count)
            pairs.append((i * lon_count + j, target[0] * lon_count + target[1]))
    return pairs


def ring_padded(block, flip_sign, band_index, lon_index, lat_count, lon_count):
    first = block[:, :, :2]
    last = block[:, :, -2:]
    far_half = lon_index >= lon_count // 2
    axes = ("lat",) + LON
    up = lax.ppermute(jnp.where(far_half, first, last), axes, ring_pairs(lat_count, lon_count, True))
    down = lax.ppermute(jnp.where(far_half, last, first), axes, ring_pairs(lat_count, lon_count, False))
    south = jnp.where(far_half, down, up)
    north = jnp.where(far_half, up, down)
    zero = jnp.zeros_like(south[:, :, :1])
    south_pole = jnp.concatenate([zero, flip_sign * south[:, :, :1]], axis=2)
    north_pole = jnp.concatenate([flip_sign * north[:, :, 1:], zero], axis=2)
    south = jnp.where(band_index == 0, south_pole, south)
    north = jnp.where(band_index == lat_count - 1, north_pole, north)
    return jnp.concatenate([south, block, north], axis=2)


def lon_halos(block, lon_index, lon_count):
    first = block[..., :2]
    last = block[..., -2:]
    odd = lon_index % 2 == 1
    across = [(j, (j + 1) % lon_count if j % 2 else (j - 1) % lon_count) for j in range(lon_count)]
    far = lax.ppermute(jnp.where(odd, last, first), LON, across)
    near = lax.ppermute(jnp.where(odd, first, last), LON, [(j, j ^ 1) for j in range(lon_count)])
    west = jnp.where(odd, near, far)
    east = jnp.where(odd, far, near)
    return jnp.concatenate([west, block, east], axis=3)


def local(base_state, section_state, cutoff, filter_mask):
    fields, levels, row_count, col_count = section_state.shape
    lat_count = lax.axis_size("lat")
    lon_count = lax.axis_size(LON)
    lon_index = lax.axis_index(LON)
    band_index = lax.axis_index("lat")
    total_rows = row_count * lat_count
    total_cols = col_count * lon_count
    first_row = band_index * row_count
    flip_sign = jnp.where(jnp.arange(fields) < 2, -1.0, 1.0).astype(jnp.float32)[:, None, None, None]
    lat_padded = ring_padded(section_state, flip_sign, band_index, lon_index, lat_count, lon_count)
    lon_padded = lon_halos(section_state, lon_index, lon_count)
    face_cos = face_cosine(first_row, row_count, total_rows)
    cell_cos = cell_cosine(first_row, row_count, total_rows)
    lat_faces = interface(lat_padded, 2)
    lon_faces = interface(lon_padded, 3)
    north_flux = lat_faces[1][None] * lat_faces * face_cos[None, None, :, None]
    east_flux = lon_faces[0][None] * lon_faces
    tendency = (
        -(east_flux[..., 1:] - east_flux[..., :-1] + (north_flux[:, :, 1:] - north_flux[:, :, :-1]))
        / cell_cos[None, None, :, None]
    )
    own_mask = lax.dynamic_slice_in_dim(filter_mask, first_row, row_count)
    cut_rows = lax.dynamic_slice_in_dim(cutoff, first_row, row_count)
    smooth = run_filter(tendency, cut_rows, lon_index * col_count, total_cols)
    filtered = jnp.where(own_mask[None, None, :, None] == 1, smooth, tendency)
    return base_state + section_weight * filtered


def solution(mesh):
    rings = mesh.shape["lon"] // 4
    mesh = jax.sharding.Mesh(mesh.devices.reshape(mesh.shape["lat"], rings, 2, 2), ("lat",) + LON)
    placed = (P(None, None, "lat", LON), P(None, None, "lat", LON), P(), P())
    return jax.shard_map(
        local, mesh=mesh, in_specs=placed, out_specs=P(None, None, "lat", LON), check_vma=False
    )
```
